256 devices in a mesh: sta: 16 (over z, y_lo), win: 16 (over x, y_hi, core).
Axes of the slice: x: 4, y: 4 (y_hi: 2, y_lo: 2; y = y_hi * 2 + y_lo), z: 8, core: 2. Of those that a mesh axis runs over, the one named last changes fastest.
Arguments:
- spectra: bfloat16 [16, 1024, 4096], P('win', 'sta'), may hold values from -80 to 80
- pair_first: int32 [16, 9, 48], P('sta'), may hold values from 0 to 63
- pair_second: int32 [16, 9, 48], P('sta'), may hold values from 0 to 63
- pair_owner: int32 [16, 9, 48], P('sta'), may hold values from 0 to 15, as said below
Outputs:
- correlations: bfloat16 [16, 864, 1024], P('sta', 'win')
The draws below stay inside these ranges and needn't reach their ends.
Inputs may be any that keep to these rules, and one draw needn't show every extreme that they name: `pair_owner`: in each block row at most 54 pairs share an owner, and one owner of the row has exactly 54.
All inputs are finite; a program needn't handle non-finite values.
Results may differ from the reference program's by a relative error of at most 0.014.
Values may be sent and summed in bfloat16 or wider, within the bound.
No kernel may reach another device: no remote copies, remote signals or barrier semaphores. Data moves between devices by JAX's collectives and lax.ppermute only.
A program may use at most 64 MiB of HBM per device.

```python
import math
import jax
import jax.numpy as jnp
from jax import lax

STA_DEV = 64
WIN_DEV = 1
N_SAMP = 4096
LAGS = 1024
SMOOTH_HALF = 10
PK = 48
OFFSETS = 9
CAP = 54
STATIONS = 1024
WINDOWS = 16
N_STA = 16
N_WIN = 16


def draw_spectra(key, part):
    key_list = jax.random.split(key, 3)
    full_shape = (WINDOWS, STATIONS, N_SAMP)
    gain_value = jnp.exp(jax.random.uniform(key_list[0], (WINDOWS, STATIONS, 1), jnp.float32, math.log(0.1), math.log(10.0)))
    roughness = jnp.exp(jax.random.uniform(key_list[1], full_shape, jnp.float32, math.log(0.5), math.log(2.0)))
    values = jax.random.truncated_normal(key_list[2], -4.0, 4.0, full_shape, jnp.float32) * roughness
    return (gain_value * values).astype(jnp.bfloat16)


def draw_pair_owner(key, part):
    pair_total = OFFSETS * PK
    key_list = jax.random.split(jax.random.fold_in(key, 7), N_STA)

    def one_row(row_key):
        first_key, second_key, third_key = jax.random.split(row_key, 3)
        rank_value = jax.random.permutation(first_key, pair_total).astype(jnp.int32)
        busy_owner = jax.random.randint(second_key, (), 0, N_WIN, jnp.int32)
        turn_offset = jax.random.randint(third_key, (), 0, N_WIN - 1, jnp.int32)
        other_owner = busy_owner + 1 + jnp.mod(rank_value - CAP + turn_offset, N_WIN - 1)
        chosen = jnp.where(rank_value < CAP, busy_owner, jnp.mod(other_owner, N_WIN))
        return chosen.astype(jnp.int32).reshape(OFFSETS, PK)
    return jax.vmap(one_row)(key_list)


def plant(array, stream_key, low, top_value):
    shape = array.shape
    place = [jax.random.randint(jax.random.fold_in(stream_key, axis), (), 0, shape[axis]) for axis in range(len(shape))]
    array = array.at[tuple(place)].set(low)
    longest = shape.index(max(shape))
    place[longest] = (place[longest] + 1) % shape[longest]
    return array.at[tuple(place)].set(top_value)


def setup_inputs(seed: int = 0) -> dict:
    arg_keys = jax.random.split(jax.random.key(seed), 5)
    return {
        "spectra": draw_spectra(jax.random.fold_in(arg_keys[4], 71), 0),
        "pair_first": plant(jax.random.randint(arg_keys[1], (N_STA, OFFSETS, PK), 0, STA_DEV), jax.random.fold_in(arg_keys[1], 1), 0, STA_DEV - 1).astype(jnp.int32),
        "pair_second": plant(jax.random.randint(arg_keys[2], (N_STA, OFFSETS, PK), 0, STA_DEV), jax.random.fold_in(arg_keys[2], 1), 0, STA_DEV - 1).astype(jnp.int32),
        "pair_owner": draw_pair_owner(jax.random.fold_in(arg_keys[4], 71), 0),
    }


floor_level = 0.5

def whiten(spectra, half_width):
    bin_count = spectra.shape[-1] // 2
    real_part = spectra[..., :bin_count].astype(jnp.float32)
    imag_part = spectra[..., bin_count:].astype(jnp.float32)
    amplitude = jnp.sqrt(real_part * real_part + imag_part * imag_part)
    padded = jnp.pad(amplitude, ((0, 0), (0, 0), (half_width, half_width)))
    running = padded[..., 0:bin_count]
    for offset in range(1, 2 * half_width + 1):
        running = running + padded[..., offset:offset + bin_count]
    smooth = running / (2 * half_width + 1)
    inverse = 1.0 / jnp.maximum(smooth, floor_level)
    return jnp.concatenate([real_part * inverse, imag_part * inverse], axis=-1).astype(jnp.bfloat16)

def cross_rows(own_block, other_block, first_index, second_index):
    bin_count = own_block.shape[-1] // 2
    left_rows = jnp.take(own_block, first_index, axis=1).astype(jnp.float32)
    right_rows = jnp.take(other_block, second_index, axis=1).astype(jnp.float32)
    left_real, left_imag = (left_rows[..., :bin_count], left_rows[..., bin_count:])
    right_real, right_imag = (right_rows[..., :bin_count], right_rows[..., bin_count:])
    real_cross = left_real * right_real + left_imag * right_imag
    imag_cross = left_imag * right_real - left_real * right_imag
    return lax.optimization_barrier(jnp.sum(jnp.concatenate([real_cross, imag_cross], axis=-1), axis=0))

def owner_slots(owners, groups):
    flat_owner = owners.reshape(-1)
    owner_hits = (flat_owner[:, None] == jnp.arange(groups, dtype=jnp.int32)[None, :]).astype(jnp.int32)
    before = jnp.cumsum(owner_hits, axis=0) - owner_hits
    return (flat_owner, lax.optimization_barrier(jnp.sum(before * owner_hits, axis=1)).astype(jnp.int32))

def lag_table(bin_count, lag_count, row_start, rows):
    row_index = row_start + jnp.arange(rows, dtype=jnp.int32)
    frequency = row_index % bin_count
    lag_value = jnp.arange(lag_count, dtype=jnp.int32) - lag_count // 2
    phase_step = jnp.mod(frequency[:, None] * lag_value[None, :], 2 * bin_count)
    angle_value = phase_step.astype(jnp.float32) * (2.0 * math.pi / (2 * bin_count))
    weight = jnp.where(frequency == 0, 1.0, 2.0).astype(jnp.float32)[:, None]
    values = jnp.where((row_index < bin_count)[:, None], jnp.cos(angle_value), -jnp.sin(angle_value)) * weight
    return values.astype(jnp.bfloat16)

def transform(stacked, table, factor):
    return (jnp.dot(stacked, table, preferred_element_type=jnp.float32) * factor).astype(jnp.bfloat16)

def reference(spectra, pair_first, pair_second, pair_owner):

    def whiten_window(window_data):
        return whiten(window_data[None], SMOOTH_HALF)[0]
    whitened = lax.map(whiten_window, spectra)
    grouped = whitened.reshape(N_WIN, WIN_DEV, N_STA, STA_DEV, N_SAMP)
    table = lag_table(N_SAMP // 2, LAGS, 0, N_SAMP)
    factor = 1.0 / math.sqrt(N_SAMP * WINDOWS)
    offsets = N_STA // 2 + 1

    def one_row(block_row):
        first_rows = jnp.take(pair_first, block_row, axis=0)
        second_rows = jnp.take(pair_second, block_row, axis=0)
        owner_row = jnp.take(pair_owner, block_row, axis=0)
        own_block = jnp.take(grouped, block_row, axis=2)
        pieces = []
        for offset_step in range(offsets):
            partner = ((block_row + offset_step) % N_STA).astype(jnp.int32)
            other_block = jnp.take(grouped, partner, axis=2)

            def per_group(own_group, other_group):
                return cross_rows(own_group, other_group, first_rows[offset_step], second_rows[offset_step])
            pieces.append(jax.vmap(per_group)(own_block, other_block).astype(jnp.bfloat16))
        partial_value = jnp.concatenate(pieces, axis=1)
        stacked = lax.optimization_barrier(jnp.sum(partial_value.astype(jnp.float32), axis=0)).astype(jnp.bfloat16)
        correlated = transform(stacked, table, factor)
        owners, slot_of = owner_slots(owner_row, N_WIN)
        target = owners * CAP + slot_of
        return jnp.zeros((N_WIN * CAP, LAGS), jnp.bfloat16).at[target].set(correlated)
    return lax.map(one_row, jnp.arange(N_STA, dtype=jnp.int32))
```

```python
import math

import jax
import jax.numpy as jnp
from jax import lax
from jax.sharding import PartitionSpec as P

LAGS = 1024
SMOOTH_HALF = 10


floor_level = 0.5


def shifted(value, axis, pairs):
    return lax.ppermute(value, axis, pairs)


def whiten(spectra, half_width):
    bin_count = spectra.shape[-1] // 2
    real_part = spectra[..., :bin_count].astype(jnp.float32)
    imag_part = spectra[..., bin_count:].astype(jnp.float32)
    amplitude = jnp.sqrt(real_part * real_part + imag_part * imag_part)
    padded = jnp.pad(amplitude, ((0, 0), (half_width, half_width)))
    running = padded[..., 0:bin_count]
    for offset in range(1, 2 * half_width + 1):
        running = running + padded[..., offset : offset + bin_count]
    smooth = running / (2 * half_width + 1)
    inverse = 1.0 / jnp.maximum(smooth, floor_level)
    return jnp.concatenate([real_part * inverse, imag_part * inverse], axis=-1).astype(jnp.bfloat16)


def cross_rows(own_block, other_block, first_index, second_index):
    bin_count = own_block.shape[-1] // 2
    left_rows = jnp.take(own_block, first_index, axis=0).astype(jnp.float32)
    right_rows = jnp.take(other_block, second_index, axis=0).astype(jnp.float32)
    left_real, left_imag = (left_rows[..., :bin_count], left_rows[..., bin_count:])
    right_real, right_imag = (right_rows[..., :bin_count], right_rows[..., bin_count:])
    real_cross = left_real * right_real + left_imag * right_imag
    imag_cross = left_imag * right_real - left_real * right_imag
    return jnp.concatenate([real_cross, imag_cross], axis=-1).astype(jnp.bfloat16)


def owner_slots(owners, groups):
    flat_owner = owners.reshape(-1)
    owner_hits = (flat_owner[:, None] == jnp.arange(groups, dtype=jnp.int32)[None, :]).astype(
        jnp.int32
    )
    before = jnp.cumsum(owner_hits, axis=0) - owner_hits
    return (flat_owner, jnp.sum(before * owner_hits, axis=1))


def angle_tables(count, step, lag_count):
    period = 2 * 2048
    lag_value = jnp.arange(lag_count, dtype=jnp.int32) - lag_count // 2
    m = jnp.arange(count, dtype=jnp.int32)
    phase = jnp.mod((m * step)[:, None] * lag_value[None, :], period)
    angle = phase.astype(jnp.float32) * (2.0 * math.pi / period)
    return jnp.cos(angle), jnp.sin(angle)


def build_table(bin_count, lag_count):
    hi_step = 64
    hi_count = bin_count // hi_step
    cos_hi, sin_hi = angle_tables(hi_count, hi_step, lag_count)
    cos_lo, sin_lo = angle_tables(hi_step, 1, lag_count)
    cos_full = cos_hi[:, None, :] * cos_lo[None, :, :] - sin_hi[:, None, :] * sin_lo[None, :, :]
    sin_full = sin_hi[:, None, :] * cos_lo[None, :, :] + cos_hi[:, None, :] * sin_lo[None, :, :]
    cos_full = cos_full.reshape(bin_count, lag_count)
    sin_full = sin_full.reshape(bin_count, lag_count)
    frequency = jnp.arange(bin_count, dtype=jnp.int32)
    weight = jnp.where(frequency == 0, 1.0, 2.0).astype(jnp.float32)[:, None]
    return jnp.concatenate([cos_full * weight, -sin_full * weight], axis=0).astype(jnp.bfloat16)


def local(spectra, pair_first, pair_second, pair_owner):
    groups = lax.axis_size("win")
    peers = lax.axis_size("sta")
    bin_count = spectra.shape[-1] // 2
    windows_all = spectra.shape[0] * groups
    factor = 1.0 / math.sqrt(2 * bin_count * windows_all)
    whitened = whiten(spectra[0], SMOOTH_HALF)
    first_rows = pair_first[0]
    second_rows = pair_second[0]
    offsets = first_rows.shape[0]
    me = lax.axis_index("sta")
    is_odd = (me % 2) == 1

    z_pairs = [(i, (i - 2) % peers) for i in range(peers)]
    y_pairs = [(i, i ^ 1) for i in range(peers)]
    rounds = offsets // 2
    chain = [whitened]
    for _ in range(rounds):
        chain.append(shifted(chain[-1], "sta", z_pairs))
    blocks = [None] * offsets
    for r in range(rounds + 1):
        blocks[2 * r] = chain[r]
    for m in range(rounds):
        outgoing_block = jnp.where(is_odd, chain[m], chain[m + 1])
        blocks[2 * m + 1] = shifted(outgoing_block, "sta", y_pairs)

    table = build_table(bin_count, LAGS)
    pieces = []
    for offset_step in range(offsets):
        pieces.append(
            cross_rows(
                whitened, blocks[offset_step], first_rows[offset_step], second_rows[offset_step]
            )
        )
    partial_value = jnp.concatenate(pieces, axis=0)
    transformed = (
        jnp.dot(partial_value, table, preferred_element_type=jnp.float32) * factor
    ).astype(jnp.bfloat16)
    pair_rows = partial_value.shape[0]
    capacity = 2 * pair_rows // groups
    owners, slot_of = owner_slots(pair_owner[0], groups)
    target = owners * capacity + slot_of
    placement = (
        target[None, :] == jnp.arange(groups * capacity, dtype=jnp.int32)[:, None]
    ).astype(jnp.bfloat16)
    outgoing = jnp.dot(placement, transformed, preferred_element_type=jnp.float32).astype(
        jnp.bfloat16
    )
    outgoing = outgoing.reshape(groups, capacity, LAGS)
    received = lax.all_to_all(outgoing, "win", split_axis=0, concat_axis=0, tiled=True)
    result = jnp.sum(received.astype(jnp.float32), axis=0).astype(jnp.bfloat16)
    return result[None]


def solution(mesh):
    placed = (
        P("win", "sta", None),
        P("sta", None, None),
        P("sta", None, None),
        P("sta", None, None),
    )
    return jax.shard_map(
        local, mesh=mesh, in_specs=placed, out_specs=P("sta", "win", None), check_vma=False
    )
```

```python
import math

import jax
import jax.numpy as jnp
from jax import lax
from jax.sharding import Mesh, PartitionSpec as P

LAGS = 1024
SMOOTH_HALF = 10


floor_level = 0.5


def shifted(value, axis, pairs):
    return lax.ppermute(value, axis, pairs)


def whiten(spectra, half_width):
    bin_count = spectra.shape[-1] // 2
    real_part = spectra[..., :bin_count].astype(jnp.float32)
    imag_part = spectra[..., bin_count:].astype(jnp.float32)
    amplitude = jnp.sqrt(real_part * real_part + imag_part * imag_part)
    padded = jnp.pad(amplitude, ((0, 0), (half_width, half_width)))
    running = padded[..., 0:bin_count]
    for offset in range(1, 2 * half_width + 1):
        running = running + padded[..., offset : offset + bin_count]
    smooth = running / (2 * half_width + 1)
    inverse = 1.0 / jnp.maximum(smooth, floor_level)
    return jnp.concatenate([real_part * inverse, imag_part * inverse], axis=-1).astype(jnp.bfloat16)


def owner_slots(owners, groups):
    flat_owner = owners.reshape(-1)
    owner_hits = (flat_owner[:, None] == jnp.arange(groups, dtype=jnp.int32)[None, :]).astype(
        jnp.int32
    )
    before = jnp.cumsum(owner_hits, axis=0) - owner_hits
    return (flat_owner, jnp.sum(before * owner_hits, axis=1))


def angle_tables(count, step, lag_count):
    period = 2 * 2048
    lag_value = jnp.arange(lag_count, dtype=jnp.int32) - lag_count // 2
    m = jnp.arange(count, dtype=jnp.int32)
    phase = jnp.mod((m * step)[:, None] * lag_value[None, :], period)
    angle = phase.astype(jnp.float32) * (2.0 * math.pi / period)
    return jnp.cos(angle), jnp.sin(angle)


def build_table(bin_count, lag_count):
    hi_step = 64
    hi_count = bin_count // hi_step
    cos_hi, sin_hi = angle_tables(hi_count, hi_step, lag_count)
    cos_lo, sin_lo = angle_tables(hi_step, 1, lag_count)
    cos_full = cos_hi[:, None, :] * cos_lo[None, :, :] - sin_hi[:, None, :] * sin_lo[None, :, :]
    sin_full = sin_hi[:, None, :] * cos_lo[None, :, :] + cos_hi[:, None, :] * sin_lo[None, :, :]
    cos_full = cos_full.reshape(bin_count, lag_count)
    sin_full = sin_full.reshape(bin_count, lag_count)
    frequency = jnp.arange(bin_count, dtype=jnp.int32)
    weight = jnp.where(frequency == 0, 1.0, 2.0).astype(jnp.float32)[:, None]
    return jnp.concatenate([cos_full * weight, -sin_full * weight], axis=0).astype(jnp.bfloat16)


def select_rows(index, block):
    count = block.shape[0]
    chooser = (index[:, None] == jnp.arange(count, dtype=jnp.int32)[None, :]).astype(block.dtype)
    return jnp.dot(chooser, block, preferred_element_type=jnp.float32)


def cross_rows(left_rows, right_rows):
    bin_count = left_rows.shape[-1] // 2
    left_real, left_imag = (left_rows[..., :bin_count], left_rows[..., bin_count:])
    right_real, right_imag = (right_rows[..., :bin_count], right_rows[..., bin_count:])
    real_cross = left_real * right_real + left_imag * right_imag
    imag_cross = left_imag * right_real - left_real * right_imag
    return jnp.concatenate([real_cross, imag_cross], axis=-1).astype(jnp.bfloat16)


def local(spectra, pair_first, pair_second, pair_owner):
    chips = lax.axis_size("wx")
    cores = lax.axis_size("wc")
    groups = chips * cores
    peers = lax.axis_size("sta")
    bin_count = spectra.shape[-1] // 2
    windows_all = spectra.shape[0] * groups
    factor = 1.0 / math.sqrt(2 * bin_count * windows_all)
    whitened = whiten(spectra[0], SMOOTH_HALF)
    first_rows = pair_first[0]
    second_rows = pair_second[0]
    offsets = first_rows.shape[0]

    z_pairs = [(i, (i - 2) % peers) for i in range(peers)]
    to_even = [(i, i - 1) for i in range(1, peers, 2)]
    to_odd = [(i, i + 1) for i in range(0, peers, 2)]
    rounds = offsets // 2
    chain = [whitened]
    for _ in range(rounds):
        chain.append(shifted(chain[-1], "sta", z_pairs))
    partner_rows = [None] * offsets
    for r in range(rounds + 1):
        partner_rows[2 * r] = select_rows(second_rows[2 * r], chain[r])
    for m in range(rounds):
        from_odd = shifted(chain[m], "sta", to_even)
        from_even = shifted(chain[m + 1], "sta", to_odd)
        partner_rows[2 * m + 1] = select_rows(second_rows[2 * m + 1], from_odd) + select_rows(
            second_rows[2 * m + 1], from_even
        )

    table = build_table(bin_count, LAGS)
    pieces = []
    for offset_step in range(offsets):
        own_rows = select_rows(first_rows[offset_step], whitened)
        pieces.append(cross_rows(own_rows, partner_rows[offset_step]))
    partial_value = jnp.concatenate(pieces, axis=0)
    transformed = (
        jnp.dot(partial_value, table, preferred_element_type=jnp.float32) * factor
    ).astype(jnp.bfloat16)
    pair_rows = partial_value.shape[0]
    capacity = 2 * pair_rows // groups
    owners, slot_of = owner_slots(pair_owner[0], groups)
    target = owners * capacity + slot_of
    placement = (
        target[None, :] == jnp.arange(groups * capacity, dtype=jnp.int32)[:, None]
    ).astype(jnp.bfloat16)
    outgoing = jnp.dot(placement, transformed, preferred_element_type=jnp.float32).astype(
        jnp.bfloat16
    )
    outgoing = outgoing.reshape(chips, cores, capacity, LAGS)
    on_chip = lax.all_to_all(outgoing, "wc", split_axis=1, concat_axis=1, tiled=True)
    chip_sum = jnp.sum(on_chip.astype(jnp.float32), axis=1).astype(jnp.bfloat16)
    received = lax.all_to_all(chip_sum, "wx", split_axis=0, concat_axis=0, tiled=True)
    result = jnp.sum(received.astype(jnp.float32), axis=0).astype(jnp.bfloat16)
    return result[None]


def solution(mesh):
    sta_count, win_count = mesh.devices.shape
    split_mesh = Mesh(mesh.devices.reshape(sta_count, win_count // 2, 2), ("sta", "wx", "wc"))
    win = ("wx", "wc")
    placed = (
        P(win, "sta", None),
        P("sta", None, None),
        P("sta", None, None),
        P("sta", None, None),
    )
    return jax.shard_map(
        local, mesh=split_mesh, in_specs=placed, out_specs=P("sta", win, None), check_vma=False
    )
```

```python
import math

import jax
import jax.numpy as jnp
from jax import lax
from jax.sharding import Mesh, PartitionSpec as P

LAGS = 1024
SMOOTH_HALF = 10


floor_level = 0.5


def shifted(value, axis, pairs):
    return lax.ppermute(value, axis, pairs)


def whiten(spectra, half_width):
    bin_count = spectra.shape[-1] // 2
    real_part = spectra[..., :bin_count].astype(jnp.float32)
    imag_part = spectra[..., bin_count:].astype(jnp.float32)
    amplitude = jnp.sqrt(real_part * real_part + imag_part * imag_part)
    padded = jnp.pad(amplitude, ((0, 0), (half_width, half_width)))
    running = padded[..., 0:bin_count]
    for offset in range(1, 2 * half_width + 1):
        running = running + padded[..., offset : offset + bin_count]
    smooth = running / (2 * half_width + 1)
    inverse = 1.0 / jnp.maximum(smooth, floor_level)
    return jnp.concatenate([real_part * inverse, imag_part * inverse], axis=-1).astype(jnp.bfloat16)


def owner_slots(owners, groups):
    flat_owner = owners.reshape(-1)
    count = flat_owner.shape[0]
    owner_hits = (flat_owner[:, None] == jnp.arange(groups, dtype=jnp.int32)[None, :]).astype(
        jnp.bfloat16
    )
    position = jnp.arange(count, dtype=jnp.int32)
    earlier = (position[None, :] < position[:, None]).astype(jnp.bfloat16)
    before = jnp.dot(earlier, owner_hits, preferred_element_type=jnp.float32)
    slot = jnp.sum(before * owner_hits.astype(jnp.float32), axis=1).astype(jnp.int32)
    return (flat_owner, slot)


def angle_tables(count, step, lag_count):
    period = 2 * 2048
    lag_value = jnp.arange(lag_count, dtype=jnp.int32) - lag_count // 2
    m = jnp.arange(count, dtype=jnp.int32)
    phase = jnp.mod((m * step)[:, None] * lag_value[None, :], period)
    angle = phase.astype(jnp.float32) * (2.0 * math.pi / period)
    return jnp.cos(angle), jnp.sin(angle)


def build_table(bin_count, lag_count):
    hi_step = 64
    hi_count = bin_count // hi_step
    cos_hi, sin_hi = angle_tables(hi_count, hi_step, lag_count)
    cos_lo, sin_lo = angle_tables(hi_step, 1, lag_count)
    frequency = jnp.arange(bin_count, dtype=jnp.int32).reshape(hi_count, hi_step, 1)
    weight = jnp.where(frequency == 0, 1.0, 2.0).astype(jnp.float32)
    cos_full = (cos_hi[:, None, :] * cos_lo[None, :, :] - sin_hi[:, None, :] * sin_lo[None, :, :]) * weight
    sin_full = (sin_hi[:, None, :] * cos_lo[None, :, :] + cos_hi[:, None, :] * sin_lo[None, :, :]) * weight
    table = jnp.stack([cos_full, -sin_full]).astype(jnp.bfloat16)
    return table.reshape(2 * bin_count, lag_count)


def select_rows(index, block):
    count = block.shape[0]
    chooser = (index[:, None] == jnp.arange(count, dtype=jnp.int32)[None, :]).astype(block.dtype)
    return jnp.dot(chooser, block, preferred_element_type=jnp.float32).astype(block.dtype)


def cross_rows(left_rows, right_rows):
    bin_count = left_rows.shape[-1] // 2
    left_real, left_imag = (left_rows[..., :bin_count], left_rows[..., bin_count:])
    right_real, right_imag = (right_rows[..., :bin_count], right_rows[..., bin_count:])
    real_cross = left_real * right_real + left_imag * right_imag
    imag_cross = left_imag * right_real - left_real * right_imag
    return jnp.concatenate([real_cross, imag_cross], axis=-1).astype(jnp.bfloat16)


def local(spectra, pair_first, pair_second, pair_owner):
    chips = lax.axis_size("wx")
    cores = lax.axis_size("wc")
    groups = chips * cores
    peers = lax.axis_size("sta")
    bin_count = spectra.shape[-1] // 2
    windows_all = spectra.shape[0] * groups
    factor = 1.0 / math.sqrt(2 * bin_count * windows_all)
    whitened = whiten(spectra[0], SMOOTH_HALF)
    first_rows = pair_first[0]
    second_rows = pair_second[0]
    offsets = first_rows.shape[0]

    z_pairs = [(i, (i - 2) % peers) for i in range(peers)]
    to_even = [(i, i - 1) for i in range(1, peers, 2)]
    to_odd = [(i, i + 1) for i in range(0, peers, 2)]
    rounds = offsets // 2
    chain = [whitened]
    for _ in range(rounds):
        chain.append(shifted(chain[-1], "sta", z_pairs))
    partner_rows = [None] * offsets
    for r in range(rounds + 1):
        partner_rows[2 * r] = select_rows(second_rows[2 * r], chain[r])
    for m in range(rounds):
        from_odd = shifted(chain[m], "sta", to_even)
        from_even = shifted(chain[m + 1], "sta", to_odd)
        partner_rows[2 * m + 1] = select_rows(second_rows[2 * m + 1], from_odd).astype(
            jnp.float32
        ) + select_rows(second_rows[2 * m + 1], from_even).astype(jnp.float32)

    table = build_table(bin_count, LAGS)
    pair_count = first_rows.shape[1]
    own_all = select_rows(first_rows.reshape(-1), whitened)
    pieces = []
    for offset_step in range(offsets):
        own_rows = own_all[offset_step * pair_count : (offset_step + 1) * pair_count]
        pieces.append(
            cross_rows(own_rows.astype(jnp.float32), partner_rows[offset_step].astype(jnp.float32))
        )
    partial_value = jnp.concatenate(pieces, axis=0)
    transformed = (
        jnp.dot(partial_value, table, preferred_element_type=jnp.float32) * factor
    ).astype(jnp.bfloat16)
    pair_rows = partial_value.shape[0]
    capacity = 2 * pair_rows // groups
    owner_row, _ = lax.optimization_barrier((pair_owner[0], chain[2]))
    owners, slot_of = owner_slots(owner_row, groups)
    target = owners * capacity + slot_of
    placement = (
        target[None, :] == jnp.arange(groups * capacity, dtype=jnp.int32)[:, None]
    ).astype(jnp.bfloat16)
    outgoing = jnp.dot(placement, transformed, preferred_element_type=jnp.float32).astype(
        jnp.bfloat16
    )
    outgoing = outgoing.reshape(chips, cores, capacity, LAGS)
    on_chip = lax.all_to_all(outgoing, "wc", split_axis=1, concat_axis=1, tiled=True)
    chip_sum = jnp.sum(on_chip.astype(jnp.float32), axis=1).astype(jnp.bfloat16)
    received = lax.all_to_all(chip_sum, "wx", split_axis=0, concat_axis=0, tiled=True)
    result = jnp.sum(received.astype(jnp.float32), axis=0).astype(jnp.bfloat16)
    return result[None]


def solution(mesh):
    sta_count, win_count = mesh.devices.shape
    split_mesh = Mesh(mesh.devices.reshape(sta_count, win_count // 2, 2), ("sta", "wx", "wc"))
    win = ("wx", "wc")
    placed = (
        P(win, "sta", None),
        P("sta", None, None),
        P("sta", None, None),
        P("sta", None, None),
    )
    return jax.shard_map(
        local, mesh=split_mesh, in_specs=placed, out_specs=P("sta", win, None), check_vma=False
    )
```

```python
import math

import jax
import jax.numpy as jnp
from jax import lax
from jax.sharding import Mesh, PartitionSpec as P

LAGS = 1024
SMOOTH_HALF = 10


floor_level = 0.5


def shifted(value, axis, pairs):
    return lax.ppermute(value, axis, pairs)


def whiten(spectra, half_width):
    bin_count = spectra.shape[-1] // 2
    real_part = spectra[..., :bin_count].astype(jnp.float32)
    imag_part = spectra[..., bin_count:].astype(jnp.float32)
    amplitude = jnp.sqrt(real_part * real_part + imag_part * imag_part)
    padded = jnp.pad(amplitude, ((0, 0), (half_width, half_width)))
    running = padded[..., 0:bin_count]
    for offset in range(1, 2 * half_width + 1):
        running = running + padded[..., offset : offset + bin_count]
    smooth = running / (2 * half_width + 1)
    inverse = 1.0 / jnp.maximum(smooth, floor_level)
    return jnp.concatenate([real_part * inverse, imag_part * inverse], axis=-1).astype(jnp.bfloat16)


def owner_slots(owners, groups):
    flat_owner = owners.reshape(-1)
    count = flat_owner.shape[0]
    owner_hits = (flat_owner[:, None] == jnp.arange(groups, dtype=jnp.int32)[None, :]).astype(
        jnp.bfloat16
    )
    position = jnp.arange(count, dtype=jnp.int32)
    earlier = (position[None, :] < position[:, None]).astype(jnp.bfloat16)
    before = jnp.dot(earlier, owner_hits, preferred_element_type=jnp.float32)
    slot = jnp.sum(before * owner_hits.astype(jnp.float32), axis=1).astype(jnp.int32)
    return (flat_owner, slot)


def angle_tables(count, step, lag_count):
    period = 2 * 2048
    lag_value = jnp.arange(lag_count, dtype=jnp.int32) - lag_count // 2
    m = jnp.arange(count, dtype=jnp.int32)
    phase = jnp.mod((m * step)[:, None] * lag_value[None, :], period)
    angle = phase.astype(jnp.float32) * (2.0 * math.pi / period)
    return jnp.cos(angle), jnp.sin(angle)


def build_table(bin_count, lag_count):
    hi_step = 64
    hi_count = bin_count // hi_step
    cos_hi, sin_hi = angle_tables(hi_count, hi_step, lag_count)
    cos_lo, sin_lo = angle_tables(hi_step, 1, lag_count)
    frequency = jnp.arange(bin_count, dtype=jnp.int32).reshape(1, hi_count, hi_step, 1)
    weight = jnp.where(frequency == 0, 1.0, 2.0).astype(jnp.float32)
    ch, sh = cos_hi[None, :, None, :], sin_hi[None, :, None, :]
    cl, sl = cos_lo[None, None, :, :], sin_lo[None, None, :, :]
    part = lax.broadcasted_iota(jnp.int32, (2, 1, 1, 1), 0)
    value = jnp.where(part == 0, ch * cl - sh * sl, -(sh * cl + ch * sl)) * weight
    return value.astype(jnp.bfloat16).reshape(2 * bin_count, lag_count)


def select_rows(index, block):
    count = block.shape[0]
    chooser = (index[:, None] == jnp.arange(count, dtype=jnp.int32)[None, :]).astype(block.dtype)
    return jnp.dot(chooser, block, preferred_element_type=jnp.float32).astype(block.dtype)


def cross_rows(left_rows, right_rows):
    bin_count = left_rows.shape[-1] // 2
    left_real, left_imag = (left_rows[..., :bin_count], left_rows[..., bin_count:])
    right_real, right_imag = (right_rows[..., :bin_count], right_rows[..., bin_count:])
    real_cross = left_real * right_real + left_imag * right_imag
    imag_cross = left_imag * right_real - left_real * right_imag
    return jnp.concatenate([real_cross, imag_cross], axis=-1).astype(jnp.bfloat16)


def local(spectra, pair_first, pair_second, pair_owner):
    chips = lax.axis_size("wx")
    cores = lax.axis_size("wc")
    groups = chips * cores
    peers = lax.axis_size("sta")
    bin_count = spectra.shape[-1] // 2
    windows_all = spectra.shape[0] * groups
    factor = 1.0 / math.sqrt(2 * bin_count * windows_all)
    whitened = whiten(spectra[0], SMOOTH_HALF)
    first_rows = pair_first[0]
    second_rows = pair_second[0]
    offsets = first_rows.shape[0]

    z_pairs = [(i, (i - 2) % peers) for i in range(peers)]
    to_even = [(i, i - 1) for i in range(1, peers, 2)]
    to_odd = [(i, i + 1) for i in range(0, peers, 2)]
    rounds = offsets // 2
    chain = [whitened]
    for _ in range(rounds):
        chain.append(shifted(chain[-1], "sta", z_pairs))
    partner_rows = [None] * offsets
    for r in range(rounds + 1):
        partner_rows[2 * r] = select_rows(second_rows[2 * r], chain[r])
    for m in range(rounds):
        from_odd = shifted(chain[m], "sta", to_even)
        from_even = shifted(chain[m + 1], "sta", to_odd)
        partner_rows[2 * m + 1] = select_rows(second_rows[2 * m + 1], from_odd).astype(
            jnp.float32
        ) + select_rows(second_rows[2 * m + 1], from_even).astype(jnp.float32)

    table = build_table(bin_count, LAGS)
    pair_count = first_rows.shape[1]
    own_all = select_rows(first_rows.reshape(-1), whitened)
    pieces = []
    for offset_step in range(offsets):
        own_rows = own_all[offset_step * pair_count : (offset_step + 1) * pair_count]
        pieces.append(
            cross_rows(own_rows.astype(jnp.float32), partner_rows[offset_step].astype(jnp.float32))
        )
    partial_value = jnp.concatenate(pieces, axis=0)
    transformed = (
        jnp.dot(partial_value, table, preferred_element_type=jnp.float32) * factor
    ).astype(jnp.bfloat16)
    transformed = lax.optimization_barrier(transformed)
    pair_rows = partial_value.shape[0]
    capacity = 2 * pair_rows // groups
    padded_capacity = -(-capacity // 8) * 8
    owner_row, _ = lax.optimization_barrier((pair_owner[0], chain[2]))
    owners, slot_of = owner_slots(owner_row, groups)
    target = ((owners % cores) * chips + owners // cores) * padded_capacity + slot_of
    placement = (
        target[None, :] == jnp.arange(groups * padded_capacity, dtype=jnp.int32)[:, None]
    ).astype(jnp.bfloat16)
    outgoing = jnp.dot(placement, transformed, preferred_element_type=jnp.float32).astype(
        jnp.bfloat16
    )
    outgoing = outgoing.reshape(cores, chips, padded_capacity, LAGS)
    on_chip = lax.all_to_all(outgoing, "wc", split_axis=0, concat_axis=0, tiled=True)
    chip_sum = jnp.sum(on_chip.astype(jnp.float32), axis=0).astype(jnp.bfloat16)
    received = lax.all_to_all(chip_sum, "wx", split_axis=0, concat_axis=0, tiled=True)
    result = jnp.sum(received.astype(jnp.float32), axis=0).astype(jnp.bfloat16)[:capacity]
    return result[None]


def solution(mesh):
    sta_count, win_count = mesh.devices.shape
    split_mesh = Mesh(mesh.devices.reshape(sta_count, win_count // 2, 2), ("sta", "wx", "wc"))
    win = ("wx", "wc")
    placed = (
        P(win, "sta", None),
        P("sta", None, None),
        P("sta", None, None),
        P("sta", None, None),
    )
    return jax.shard_map(
        local, mesh=split_mesh, in_specs=placed, out_specs=P("sta", win, None), check_vma=False
    )
```

```python
import math

import jax
import jax.numpy as jnp
from jax import lax
from jax.sharding import Mesh, PartitionSpec as P

LAGS = 1024
SMOOTH_HALF = 10


floor_level = 0.5


def shifted(value, axis, pairs):
    return lax.ppermute(value, axis, pairs)


def whiten(spectra, half_width):
    bin_count = spectra.shape[-1] // 2
    real_part = spectra[..., :bin_count].astype(jnp.float32)
    imag_part = spectra[..., bin_count:].astype(jnp.float32)
    amplitude = jnp.sqrt(real_part * real_part + imag_part * imag_part)
    padded = jnp.pad(amplitude, ((0, 0), (half_width, half_width)))
    running = padded[..., 0:bin_count]
    for offset in range(1, 2 * half_width + 1):
        running = running + padded[..., offset : offset + bin_count]
    smooth = running / (2 * half_width + 1)
    inverse = 1.0 / jnp.maximum(smooth, floor_level)
    return jnp.concatenate([real_part * inverse, imag_part * inverse], axis=-1).astype(jnp.bfloat16)


def owner_slots(owners, groups):
    flat_owner = owners.reshape(-1)
    count = flat_owner.shape[0]
    owner_hits = (flat_owner[:, None] == jnp.arange(groups, dtype=jnp.int32)[None, :]).astype(
        jnp.bfloat16
    )
    position = jnp.arange(count, dtype=jnp.int32)
    earlier = (position[None, :] < position[:, None]).astype(jnp.bfloat16)
    before = jnp.dot(earlier, owner_hits, preferred_element_type=jnp.float32)
    slot = jnp.sum(before * owner_hits.astype(jnp.float32), axis=1).astype(jnp.int32)
    return (flat_owner, slot)


def angle_tables(count, step, lag_count):
    period = 2 * 2048
    lag_value = jnp.arange(lag_count, dtype=jnp.int32) - lag_count // 2
    m = jnp.arange(count, dtype=jnp.int32)
    phase = jnp.mod((m * step)[:, None] * lag_value[None, :], period)
    angle = phase.astype(jnp.float32) * (2.0 * math.pi / period)
    return jnp.cos(angle), jnp.sin(angle)


def build_table(bin_count, lag_count, after):
    hi_step = 64
    hi_count = bin_count // hi_step
    cos_hi, sin_hi = angle_tables(hi_count, hi_step, lag_count)
    cos_lo, sin_lo = angle_tables(hi_step, 1, lag_count)
    cos_hi, sin_hi, cos_lo, sin_lo, _ = lax.optimization_barrier(
        (cos_hi, sin_hi, cos_lo, sin_lo, after)
    )
    frequency = jnp.arange(bin_count, dtype=jnp.int32).reshape(hi_count, hi_step, 1)
    weight = jnp.where(frequency == 0, 1.0, 2.0).astype(jnp.float32)
    cos_full = (cos_hi[:, None, :] * cos_lo[None, :, :] - sin_hi[:, None, :] * sin_lo[None, :, :]) * weight
    sin_full = (sin_hi[:, None, :] * cos_lo[None, :, :] + cos_hi[:, None, :] * sin_lo[None, :, :]) * weight
    cos_part = cos_full.astype(jnp.bfloat16).reshape(bin_count, lag_count)
    sin_part = (-sin_full).astype(jnp.bfloat16).reshape(bin_count, lag_count)
    return cos_part, sin_part


def select_rows(index, block):
    count = block.shape[0]
    chooser = (index[:, None] == jnp.arange(count, dtype=jnp.int32)[None, :]).astype(block.dtype)
    return jnp.dot(chooser, block, preferred_element_type=jnp.float32).astype(block.dtype)


def cross_rows(left_rows, right_rows):
    bin_count = left_rows.shape[-1] // 2
    left_real, left_imag = (left_rows[..., :bin_count], left_rows[..., bin_count:])
    right_real, right_imag = (right_rows[..., :bin_count], right_rows[..., bin_count:])
    real_cross = left_real * right_real + left_imag * right_imag
    imag_cross = left_imag * right_real - left_real * right_imag
    return real_cross.astype(jnp.bfloat16), imag_cross.astype(jnp.bfloat16)


def local(spectra, pair_first, pair_second, pair_owner):
    chips = lax.axis_size("wx")
    cores = lax.axis_size("wc")
    groups = chips * cores
    peers = lax.axis_size("sta")
    bin_count = spectra.shape[-1] // 2
    windows_all = spectra.shape[0] * groups
    factor = 1.0 / math.sqrt(2 * bin_count * windows_all)
    whitened = whiten(spectra[0], SMOOTH_HALF)
    first_rows = pair_first[0]
    second_rows = pair_second[0]
    offsets = first_rows.shape[0]

    z_pairs = [(i, (i - 2) % peers) for i in range(peers)]
    to_even = [(i, i - 1) for i in range(1, peers, 2)]
    to_odd = [(i, i + 1) for i in range(0, peers, 2)]
    rounds = offsets // 2
    chain = [whitened]
    for _ in range(rounds):
        chain.append(shifted(chain[-1], "sta", z_pairs))
    partner_rows = [None] * offsets
    for r in range(rounds + 1):
        partner_rows[2 * r] = select_rows(second_rows[2 * r], chain[r])
    for m in range(rounds):
        from_odd = shifted(chain[m], "sta", to_even)
        from_even = shifted(chain[m + 1], "sta", to_odd)
        partner_rows[2 * m + 1] = select_rows(second_rows[2 * m + 1], from_odd).astype(
            jnp.float32
        ) + select_rows(second_rows[2 * m + 1], from_even).astype(jnp.float32)

    cos_table, sin_table = build_table(bin_count, LAGS, chain[2])
    pair_count = first_rows.shape[1]
    own_all = select_rows(first_rows.reshape(-1), whitened)
    pieces = []
    for offset_step in range(offsets):
        own_rows = own_all[offset_step * pair_count : (offset_step + 1) * pair_count]
        pieces.append(
            cross_rows(own_rows.astype(jnp.float32), partner_rows[offset_step].astype(jnp.float32))
        )
    real_value = jnp.concatenate([piece[0] for piece in pieces], axis=0)
    imag_value = jnp.concatenate([piece[1] for piece in pieces], axis=0)
    transformed = (
        (
            jnp.dot(real_value, cos_table, preferred_element_type=jnp.float32)
            + jnp.dot(imag_value, sin_table, preferred_element_type=jnp.float32)
        )
        * factor
    ).astype(jnp.bfloat16)
    transformed = lax.optimization_barrier(transformed)
    pair_rows = real_value.shape[0]
    capacity = 2 * pair_rows // groups
    padded_capacity = -(-capacity // 8) * 8
    owner_row, _ = lax.optimization_barrier((pair_owner[0], chain[2]))
    owners, slot_of = owner_slots(owner_row, groups)
    target = ((owners % cores) * chips + owners // cores) * padded_capacity + slot_of
    placement = (
        target[None, :] == jnp.arange(groups * padded_capacity, dtype=jnp.int32)[:, None]
    ).astype(jnp.bfloat16)
    outgoing = jnp.dot(placement, transformed, preferred_element_type=jnp.float32).astype(
        jnp.bfloat16
    )
    outgoing = outgoing.reshape(cores, chips, padded_capacity, LAGS)
    on_chip = lax.all_to_all(outgoing, "wc", split_axis=0, concat_axis=0, tiled=True)
    chip_sum = jnp.sum(on_chip.astype(jnp.float32), axis=0).astype(jnp.bfloat16)
    received = lax.all_to_all(chip_sum, "wx", split_axis=0, concat_axis=0, tiled=True)
    result = jnp.sum(received.astype(jnp.float32), axis=0).astype(jnp.bfloat16)[:capacity]
    return result[None]


def solution(mesh):
    sta_count, win_count = mesh.devices.shape
    split_mesh = Mesh(mesh.devices.reshape(sta_count, win_count // 2, 2), ("sta", "wx", "wc"))
    win = ("wx", "wc")
    placed = (
        P(win, "sta", None),
        P("sta", None, None),
        P("sta", None, None),
        P("sta", None, None),
    )
    return jax.shard_map(
        local, mesh=split_mesh, in_specs=placed, out_specs=P("sta", win, None), check_vma=False
    )
```

```python
import math

import jax
import jax.numpy as jnp
from jax import lax
from jax.sharding import Mesh, PartitionSpec as P

LAGS = 1024
SMOOTH_HALF = 10


floor_level = 0.5


def shifted(value, axis, pairs):
    return lax.ppermute(value, axis, pairs)


def whiten(spectra, half_width):
    bin_count = spectra.shape[-1] // 2
    real_part = spectra[..., :bin_count].astype(jnp.float32)
    imag_part = spectra[..., bin_count:].astype(jnp.float32)
    amplitude = jnp.sqrt(real_part * real_part + imag_part * imag_part)
    padded = jnp.pad(amplitude, ((0, 0), (half_width, half_width)))
    running = padded[..., 0:bin_count]
    for offset in range(1, 2 * half_width + 1):
        running = running + padded[..., offset : offset + bin_count]
    smooth = running / (2 * half_width + 1)
    inverse = 1.0 / jnp.maximum(smooth, floor_level)
    return jnp.concatenate([real_part * inverse, imag_part * inverse], axis=-1).astype(jnp.bfloat16)


def owner_slots(owners, groups):
    flat_owner = owners.reshape(-1)
    count = flat_owner.shape[0]
    owner_hits = (flat_owner[:, None] == jnp.arange(groups, dtype=jnp.int32)[None, :]).astype(
        jnp.bfloat16
    )
    position = jnp.arange(count, dtype=jnp.int32)
    earlier = (position[None, :] < position[:, None]).astype(jnp.bfloat16)
    before = jnp.dot(earlier, owner_hits, preferred_element_type=jnp.float32)
    slot = jnp.sum(before * owner_hits.astype(jnp.float32), axis=1).astype(jnp.int32)
    return (flat_owner, slot)


def angle_tables(count, step, lag_count):
    period = 2 * 2048
    lag_value = jnp.arange(lag_count, dtype=jnp.int32) - lag_count // 2
    m = jnp.arange(count, dtype=jnp.int32)
    phase = jnp.mod((m * step)[:, None] * lag_value[None, :], period)
    angle = phase.astype(jnp.float32) * (2.0 * math.pi / period)
    return jnp.cos(angle), jnp.sin(angle)


def build_table(bin_count, lag_count, after):
    hi_step = 64
    hi_count = bin_count // hi_step
    cos_hi, sin_hi = angle_tables(hi_count, hi_step, lag_count)
    cos_lo, sin_lo = angle_tables(hi_step, 1, lag_count)
    cos_hi, sin_hi, cos_lo, sin_lo, _ = lax.optimization_barrier(
        (cos_hi, sin_hi, cos_lo, sin_lo, after)
    )
    frequency = jnp.arange(bin_count, dtype=jnp.int32).reshape(hi_count, hi_step, 1)
    weight = jnp.where(frequency == 0, 1.0, 2.0).astype(jnp.float32)
    cos_full = (cos_hi[:, None, :] * cos_lo[None, :, :] - sin_hi[:, None, :] * sin_lo[None, :, :]) * weight
    sin_full = (sin_hi[:, None, :] * cos_lo[None, :, :] + cos_hi[:, None, :] * sin_lo[None, :, :]) * weight
    cos_part = cos_full.astype(jnp.bfloat16).reshape(bin_count, lag_count)
    sin_part = (-sin_full).astype(jnp.bfloat16).reshape(bin_count, lag_count)
    return cos_part, sin_part


def select_rows(index, block):
    count = block.shape[0]
    chooser = (index[:, None] == jnp.arange(count, dtype=jnp.int32)[None, :]).astype(block.dtype)
    return jnp.dot(chooser, block, preferred_element_type=jnp.float32).astype(block.dtype)


def cross_rows(left_rows, right_rows):
    bin_count = left_rows.shape[-1] // 2
    left_real, left_imag = (left_rows[..., :bin_count], left_rows[..., bin_count:])
    right_real, right_imag = (right_rows[..., :bin_count], right_rows[..., bin_count:])
    real_cross = left_real * right_real + left_imag * right_imag
    imag_cross = left_imag * right_real - left_real * right_imag
    return real_cross.astype(jnp.bfloat16), imag_cross.astype(jnp.bfloat16)


def local(spectra, pair_first, pair_second, pair_owner):
    chips = lax.axis_size("wx")
    cores = lax.axis_size("wc")
    groups = chips * cores
    peers = lax.axis_size("sta")
    bin_count = spectra.shape[-1] // 2
    windows_all = spectra.shape[0] * groups
    factor = 1.0 / math.sqrt(2 * bin_count * windows_all)
    whitened = whiten(spectra[0], SMOOTH_HALF)
    first_rows = pair_first[0]
    second_rows = pair_second[0]
    offsets = first_rows.shape[0]

    z_pairs = [(i, (i - 2) % peers) for i in range(peers)]
    to_even = [(i, i - 1) for i in range(1, peers, 2)]
    to_odd = [(i, i + 1) for i in range(0, peers, 2)]
    rounds = offsets // 2
    chain = [whitened]
    for _ in range(rounds - 1):
        chain.append(shifted(chain[-1], "sta", z_pairs))
    half_way = [(i, (i + peers // 2) % peers) for i in range(peers)]
    chain.append(shifted(whitened, "sta", half_way))
    partner_rows = [None] * offsets
    for r in range(rounds + 1):
        partner_rows[2 * r] = select_rows(second_rows[2 * r], chain[r])
    for m in range(rounds):
        from_odd = shifted(chain[m], "sta", to_even)
        from_even = shifted(chain[m + 1], "sta", to_odd)
        partner_rows[2 * m + 1] = select_rows(second_rows[2 * m + 1], from_odd).astype(
            jnp.float32
        ) + select_rows(second_rows[2 * m + 1], from_even).astype(jnp.float32)

    cos_table, sin_table = build_table(bin_count, LAGS, chain[2])
    pair_count = first_rows.shape[1]
    own_all = select_rows(first_rows.reshape(-1), whitened)
    pieces = []
    for offset_step in range(offsets):
        own_rows = own_all[offset_step * pair_count : (offset_step + 1) * pair_count]
        pieces.append(
            cross_rows(own_rows.astype(jnp.float32), partner_rows[offset_step].astype(jnp.float32))
        )
    real_value = jnp.concatenate([piece[0] for piece in pieces], axis=0)
    imag_value = jnp.concatenate([piece[1] for piece in pieces], axis=0)
    transformed = (
        (
            jnp.dot(real_value, cos_table, preferred_element_type=jnp.float32)
            + jnp.dot(imag_value, sin_table, preferred_element_type=jnp.float32)
        )
        * factor
    ).astype(jnp.bfloat16)
    transformed = lax.optimization_barrier(transformed)
    pair_rows = real_value.shape[0]
    capacity = 2 * pair_rows // groups
    padded_capacity = -(-capacity // 8) * 8
    owner_row, _ = lax.optimization_barrier((pair_owner[0], chain[2]))
    owners, slot_of = owner_slots(owner_row, groups)
    target = ((owners % cores) * chips + owners // cores) * padded_capacity + slot_of
    placement = (
        target[None, :] == jnp.arange(groups * padded_capacity, dtype=jnp.int32)[:, None]
    ).astype(jnp.bfloat16)
    outgoing = jnp.dot(placement, transformed, preferred_element_type=jnp.float32).astype(
        jnp.bfloat16
    )
    outgoing = outgoing.reshape(cores, chips, padded_capacity, LAGS)
    on_chip = lax.all_to_all(outgoing, "wc", split_axis=0, concat_axis=0, tiled=True)
    chip_sum = jnp.sum(on_chip.astype(jnp.float32), axis=0).astype(jnp.bfloat16)
    received = lax.all_to_all(chip_sum, "wx", split_axis=0, concat_axis=0, tiled=True)
    result = jnp.sum(received.astype(jnp.float32), axis=0).astype(jnp.bfloat16)[:capacity]
    return result[None]


def solution(mesh):
    sta_count, win_count = mesh.devices.shape
    split_mesh = Mesh(mesh.devices.reshape(sta_count, win_count // 2, 2), ("sta", "wx", "wc"))
    win = ("wx", "wc")
    placed = (
        P(win, "sta", None),
        P("sta", None, None),
        P("sta", None, None),
        P("sta", None, None),
    )
    return jax.shard_map(
        local, mesh=split_mesh, in_specs=placed, out_specs=P("sta", win, None), check_vma=False
    )
```

```python
import math

import jax
import jax.numpy as jnp
from jax import lax
from jax.sharding import Mesh, PartitionSpec as P

LAGS = 1024
SMOOTH_HALF = 10


floor_level = 0.5


def shifted(value, axis, pairs):
    return lax.ppermute(value, axis, pairs)


def whiten(spectra, half_width):
    bin_count = spectra.shape[-1] // 2
    real_part = spectra[..., :bin_count].astype(jnp.float32)
    imag_part = spectra[..., bin_count:].astype(jnp.float32)
    amplitude = jnp.sqrt(real_part * real_part + imag_part * imag_part)
    padded = jnp.pad(amplitude, ((0, 0), (half_width, half_width)))
    running = padded[..., 0:bin_count]
    for offset in range(1, 2 * half_width + 1):
        running = running + padded[..., offset : offset + bin_count]
    smooth = running / (2 * half_width + 1)
    inverse = 1.0 / jnp.maximum(smooth, floor_level)
    return jnp.concatenate([real_part * inverse, imag_part * inverse], axis=-1).astype(jnp.bfloat16)


def owner_slots(owners, groups):
    flat_owner = owners.reshape(-1)
    count = flat_owner.shape[0]
    owner_hits = (flat_owner[:, None] == jnp.arange(groups, dtype=jnp.int32)[None, :]).astype(
        jnp.bfloat16
    )
    position = jnp.arange(count, dtype=jnp.int32)
    earlier = (position[None, :] < position[:, None]).astype(jnp.bfloat16)
    before = jnp.dot(earlier, owner_hits, preferred_element_type=jnp.float32)
    slot = jnp.sum(before * owner_hits.astype(jnp.float32), axis=1).astype(jnp.int32)
    return (flat_owner, slot)


def angle_tables(count, step, lag_count):
    period = 2 * 2048
    lag_value = jnp.arange(lag_count, dtype=jnp.int32) - lag_count // 2
    m = jnp.arange(count, dtype=jnp.int32)
    phase = jnp.mod((m * step)[:, None] * lag_value[None, :], period)
    angle = phase.astype(jnp.float32) * (2.0 * math.pi / period)
    return jnp.cos(angle), jnp.sin(angle)


def build_table(bin_count, lag_count, after):
    hi_step = 64
    hi_count = bin_count // hi_step
    cos_hi, sin_hi = angle_tables(hi_count, hi_step, lag_count)
    cos_lo, sin_lo = angle_tables(hi_step, 1, lag_count)
    cos_hi, sin_hi, cos_lo, sin_lo, _ = lax.optimization_barrier(
        (cos_hi, sin_hi, cos_lo, sin_lo, after)
    )
    frequency = jnp.arange(bin_count, dtype=jnp.int32).reshape(hi_count, hi_step, 1)
    weight = jnp.where(frequency == 0, 1.0, 2.0).astype(jnp.float32)
    cos_full = (cos_hi[:, None, :] * cos_lo[None, :, :] - sin_hi[:, None, :] * sin_lo[None, :, :]) * weight
    sin_full = (sin_hi[:, None, :] * cos_lo[None, :, :] + cos_hi[:, None, :] * sin_lo[None, :, :]) * weight
    cos_part = cos_full.astype(jnp.bfloat16).reshape(bin_count, lag_count)
    sin_part = (-sin_full).astype(jnp.bfloat16).reshape(bin_count, lag_count)
    return cos_part, sin_part


def select_rows(index, block):
    count = block.shape[0]
    chooser = (index[:, None] == jnp.arange(count, dtype=jnp.int32)[None, :]).astype(block.dtype)
    return jnp.dot(chooser, block, preferred_element_type=jnp.float32).astype(block.dtype)


def cross_rows(left_rows, right_rows):
    bin_count = left_rows.shape[-1] // 2
    left_real, left_imag = (left_rows[..., :bin_count], left_rows[..., bin_count:])
    right_real, right_imag = (right_rows[..., :bin_count], right_rows[..., bin_count:])
    real_cross = left_real * right_real + left_imag * right_imag
    imag_cross = left_imag * right_real - left_real * right_imag
    return real_cross.astype(jnp.bfloat16), imag_cross.astype(jnp.bfloat16)


def local(spectra, pair_first, pair_second, pair_owner):
    chips = lax.axis_size("wx")
    cores = lax.axis_size("wc")
    groups = chips * cores
    peers = lax.axis_size("sta")
    bin_count = spectra.shape[-1] // 2
    windows_all = spectra.shape[0] * groups
    factor = 1.0 / math.sqrt(2 * bin_count * windows_all)
    whitened = whiten(spectra[0], SMOOTH_HALF)
    first_rows = pair_first[0]
    second_rows = pair_second[0]
    offsets = first_rows.shape[0]

    z_pairs = [(i, (i - 2) % peers) for i in range(peers)]
    to_even = [(i, i - 1) for i in range(1, peers, 2)]
    to_odd = [(i, i + 1) for i in range(0, peers, 2)]
    rounds = offsets // 2
    chain = [whitened]
    for _ in range(rounds):
        chain.append(shifted(chain[-1], "sta", z_pairs))
    partner_rows = [None] * offsets
    for r in range(rounds + 1):
        partner_rows[2 * r] = select_rows(second_rows[2 * r], chain[r])
    table_after = None
    for m in range(rounds):
        from_odd = shifted(chain[m], "sta", to_even)
        from_even = shifted(chain[m + 1], "sta", to_odd)
        if m == 1:
            table_after = from_even
        partner_rows[2 * m + 1] = select_rows(second_rows[2 * m + 1], from_odd).astype(
            jnp.float32
        ) + select_rows(second_rows[2 * m + 1], from_even).astype(jnp.float32)

    cos_table, sin_table = build_table(bin_count, LAGS, table_after)
    pair_count = first_rows.shape[1]
    own_all = select_rows(first_rows.reshape(-1), whitened)
    pieces = []
    for offset_step in range(offsets):
        own_rows = own_all[offset_step * pair_count : (offset_step + 1) * pair_count]
        pieces.append(
            cross_rows(own_rows.astype(jnp.float32), partner_rows[offset_step].astype(jnp.float32))
        )
    real_value = jnp.concatenate([piece[0] for piece in pieces], axis=0)
    imag_value = jnp.concatenate([piece[1] for piece in pieces], axis=0)
    transformed = (
        (
            jnp.dot(real_value, cos_table, preferred_element_type=jnp.float32)
            + jnp.dot(imag_value, sin_table, preferred_element_type=jnp.float32)
        )
        * factor
    ).astype(jnp.bfloat16)
    transformed = lax.optimization_barrier(transformed)
    pair_rows = real_value.shape[0]
    capacity = 2 * pair_rows // groups
    padded_capacity = -(-capacity // 8) * 8
    owner_row, _ = lax.optimization_barrier((pair_owner[0], chain[2]))
    owners, slot_of = owner_slots(owner_row, groups)
    target = ((owners % cores) * chips + owners // cores) * padded_capacity + slot_of
    placement = (
        target[None, :] == jnp.arange(groups * padded_capacity, dtype=jnp.int32)[:, None]
    ).astype(jnp.bfloat16)
    outgoing = jnp.dot(placement, transformed, preferred_element_type=jnp.float32).astype(
        jnp.bfloat16
    )
    outgoing = outgoing.reshape(cores, chips, padded_capacity, LAGS)
    on_chip = lax.all_to_all(outgoing, "wc", split_axis=0, concat_axis=0, tiled=True)
    chip_sum = jnp.sum(on_chip.astype(jnp.float32), axis=0).astype(jnp.bfloat16)
    received = lax.all_to_all(chip_sum, "wx", split_axis=0, concat_axis=0, tiled=True)
    result = jnp.sum(received.astype(jnp.float32), axis=0).astype(jnp.bfloat16)[:capacity]
    return result[None]


def solution(mesh):
    sta_count, win_count = mesh.devices.shape
    split_mesh = Mesh(mesh.devices.reshape(sta_count, win_count // 2, 2), ("sta", "wx", "wc"))
    win = ("wx", "wc")
    placed = (
        P(win, "sta", None),
        P("sta", None, None),
        P("sta", None, None),
        P("sta", None, None),
    )
    return jax.shard_map(
        local, mesh=split_mesh, in_specs=placed, out_specs=P("sta", win, None), check_vma=False
    )
```

```python
import math

import jax
import jax.numpy as jnp
from jax import lax
from jax.sharding import Mesh, PartitionSpec as P

LAGS = 1024
SMOOTH_HALF = 10


floor_level = 0.5


def shifted(value, axis, pairs):
    return lax.ppermute(value, axis, pairs)


def whiten(spectra, half_width):
    bin_count = spectra.shape[-1] // 2
    real_part = spectra[..., :bin_count].astype(jnp.float32)
    imag_part = spectra[..., bin_count:].astype(jnp.float32)
    amplitude = jnp.sqrt(real_part * real_part + imag_part * imag_part)
    padded = jnp.pad(amplitude, ((0, 0), (half_width, half_width)))
    running = padded[..., 0:bin_count]
    for offset in range(1, 2 * half_width + 1):
        running = running + padded[..., offset : offset + bin_count]
    smooth = running / (2 * half_width + 1)
    inverse = 1.0 / jnp.maximum(smooth, floor_level)
    return jnp.concatenate([real_part * inverse, imag_part * inverse], axis=-1).astype(jnp.bfloat16)


def owner_slots(owners, groups):
    flat_owner = owners.reshape(-1)
    count = flat_owner.shape[0]
    owner_hits = (flat_owner[:, None] == jnp.arange(groups, dtype=jnp.int32)[None, :]).astype(
        jnp.bfloat16
    )
    position = jnp.arange(count, dtype=jnp.int32)
    earlier = (position[None, :] < position[:, None]).astype(jnp.bfloat16)
    before = jnp.dot(earlier, owner_hits, preferred_element_type=jnp.float32)
    slot = jnp.sum(before * owner_hits.astype(jnp.float32), axis=1).astype(jnp.int32)
    return (flat_owner, slot)


def angle_tables(count, step, lag_count):
    period = 2 * 2048
    lag_value = jnp.arange(lag_count, dtype=jnp.int32) - lag_count // 2
    m = jnp.arange(count, dtype=jnp.int32)
    phase = jnp.mod((m * step)[:, None] * lag_value[None, :], period)
    angle = phase.astype(jnp.float32) * (2.0 * math.pi / period)
    return jnp.cos(angle), jnp.sin(angle)


def build_table(bin_count, lag_count, after):
    hi_step = 64
    hi_count = bin_count // hi_step
    cos_hi, sin_hi = angle_tables(hi_count, hi_step, lag_count)
    cos_lo, sin_lo = angle_tables(hi_step, 1, lag_count)
    cos_hi, sin_hi, cos_lo, sin_lo, _ = lax.optimization_barrier(
        (cos_hi, sin_hi, cos_lo, sin_lo, after)
    )
    frequency = jnp.arange(bin_count, dtype=jnp.int32).reshape(hi_count, hi_step, 1)
    weight = jnp.where(frequency == 0, 1.0, 2.0).astype(jnp.float32)
    cos_full = (cos_hi[:, None, :] * cos_lo[None, :, :] - sin_hi[:, None, :] * sin_lo[None, :, :]) * weight
    sin_full = (sin_hi[:, None, :] * cos_lo[None, :, :] + cos_hi[:, None, :] * sin_lo[None, :, :]) * weight
    cos_part = cos_full.astype(jnp.bfloat16).reshape(bin_count, lag_count)
    sin_part = (-sin_full).astype(jnp.bfloat16).reshape(bin_count, lag_count)
    return cos_part, sin_part


def select_rows(index, block):
    count = block.shape[0]
    chooser = (index[:, None] == jnp.arange(count, dtype=jnp.int32)[None, :]).astype(block.dtype)
    return jnp.dot(chooser, block, preferred_element_type=jnp.float32).astype(block.dtype)


def cross_rows(left_rows, right_rows):
    bin_count = left_rows.shape[-1] // 2
    left_real, left_imag = (left_rows[..., :bin_count], left_rows[..., bin_count:])
    right_real, right_imag = (right_rows[..., :bin_count], right_rows[..., bin_count:])
    real_cross = left_real * right_real + left_imag * right_imag
    imag_cross = left_imag * right_real - left_real * right_imag
    return real_cross.astype(jnp.bfloat16), imag_cross.astype(jnp.bfloat16)


def local(spectra, pair_first, pair_second, pair_owner):
    chips = lax.axis_size("wx")
    cores = lax.axis_size("wc")
    groups = chips * cores
    peers = lax.axis_size("sta")
    bin_count = spectra.shape[-1] // 2
    windows_all = spectra.shape[0] * groups
    factor = 1.0 / math.sqrt(2 * bin_count * windows_all)
    whitened = whiten(spectra[0], SMOOTH_HALF)
    first_rows = pair_first[0]
    second_rows = pair_second[0]
    offsets = first_rows.shape[0]

    z_pairs = [(i, (i - 2) % peers) for i in range(peers)]
    to_even = [(i, i - 1) for i in range(1, peers, 2)]
    to_odd = [(i, i + 1) for i in range(0, peers, 2)]
    rounds = offsets // 2
    chain = [whitened]
    for _ in range(rounds):
        chain.append(shifted(chain[-1], "sta", z_pairs))
    partner_rows = [None] * offsets
    for r in range(rounds + 1):
        partner_rows[2 * r] = select_rows(second_rows[2 * r], chain[r])
    table_after = None
    for m in range(rounds):
        from_odd = shifted(chain[m], "sta", to_even)
        from_even = shifted(chain[m + 1], "sta", to_odd)
        if m == 1:
            table_after = from_even
        partner_rows[2 * m + 1] = select_rows(second_rows[2 * m + 1], from_odd).astype(
            jnp.float32
        ) + select_rows(second_rows[2 * m + 1], from_even).astype(jnp.float32)

    cos_table, sin_table = build_table(bin_count, LAGS, table_after)
    pair_count = first_rows.shape[1]
    own_all = select_rows(first_rows.reshape(-1), whitened)
    pieces = []
    for offset_step in range(offsets):
        own_rows = own_all[offset_step * pair_count : (offset_step + 1) * pair_count]
        pieces.append(
            cross_rows(own_rows.astype(jnp.float32), partner_rows[offset_step].astype(jnp.float32))
        )
    def transform(parts):
        real_value = jnp.concatenate([piece[0] for piece in parts], axis=0)
        imag_value = jnp.concatenate([piece[1] for piece in parts], axis=0)
        value = (
            jnp.dot(real_value, cos_table, preferred_element_type=jnp.float32)
            + jnp.dot(imag_value, sin_table, preferred_element_type=jnp.float32)
        ) * factor
        return lax.optimization_barrier(value.astype(jnp.bfloat16))

    late_steps = [offsets - 2, offsets - 1]
    early_steps = [k for k in range(offsets) if k not in late_steps]
    transformed_early = transform([pieces[k] for k in early_steps])
    transformed_late = transform([pieces[k] for k in late_steps])
    pair_rows = offsets * pair_count
    capacity = 2 * pair_rows // groups
    padded_capacity = -(-capacity // 8) * 8
    owner_row, _ = lax.optimization_barrier((pair_owner[0], chain[2]))
    owners, slot_of = owner_slots(owner_row, groups)
    target = ((owners % cores) * chips + owners // cores) * padded_capacity + slot_of
    slot_index = jnp.arange(groups * padded_capacity, dtype=jnp.int32)[:, None]
    early_target = jnp.concatenate(
        [target[k * pair_count : (k + 1) * pair_count] for k in early_steps]
    )
    late_target = jnp.concatenate(
        [target[k * pair_count : (k + 1) * pair_count] for k in late_steps]
    )
    outgoing = (
        jnp.dot(
            (early_target[None, :] == slot_index).astype(jnp.bfloat16),
            transformed_early,
            preferred_element_type=jnp.float32,
        )
        + jnp.dot(
            (late_target[None, :] == slot_index).astype(jnp.bfloat16),
            transformed_late,
            preferred_element_type=jnp.float32,
        )
    ).astype(jnp.bfloat16)
    outgoing = outgoing.reshape(cores, chips, padded_capacity, LAGS)
    on_chip = lax.all_to_all(outgoing, "wc", split_axis=0, concat_axis=0, tiled=True)
    chip_sum = jnp.sum(on_chip.astype(jnp.float32), axis=0).astype(jnp.bfloat16)
    received = lax.all_to_all(chip_sum, "wx", split_axis=0, concat_axis=0, tiled=True)
    result = jnp.sum(received.astype(jnp.float32), axis=0).astype(jnp.bfloat16)[:capacity]
    return result[None]


def solution(mesh):
    sta_count, win_count = mesh.devices.shape
    split_mesh = Mesh(mesh.devices.reshape(sta_count, win_count // 2, 2), ("sta", "wx", "wc"))
    win = ("wx", "wc")
    placed = (
        P(win, "sta", None),
        P("sta", None, None),
        P("sta", None, None),
        P("sta", None, None),
    )
    return jax.shard_map(
        local, mesh=split_mesh, in_specs=placed, out_specs=P("sta", win, None), check_vma=False
    )
```

```python
import math

import jax
import jax.numpy as jnp
from jax import lax
from jax.sharding import Mesh, PartitionSpec as P

LAGS = 1024
SMOOTH_HALF = 10


floor_level = 0.5


def shifted(value, axis, pairs):
    return lax.ppermute(value, axis, pairs)


def whiten(spectra, half_width):
    bin_count = spectra.shape[-1] // 2
    real_part = spectra[..., :bin_count].astype(jnp.float32)
    imag_part = spectra[..., bin_count:].astype(jnp.float32)
    amplitude = jnp.sqrt(real_part * real_part + imag_part * imag_part)
    padded = jnp.pad(amplitude, ((0, 0), (half_width, half_width)))
    running = padded[..., 0:bin_count]
    for offset in range(1, 2 * half_width + 1):
        running = running + padded[..., offset : offset + bin_count]
    smooth = running / (2 * half_width + 1)
    inverse = 1.0 / jnp.maximum(smooth, floor_level)
    return jnp.concatenate([real_part * inverse, imag_part * inverse], axis=-1).astype(jnp.bfloat16)


def owner_slots(owners, groups):
    flat_owner = owners.reshape(-1)
    count = flat_owner.shape[0]
    owner_hits = (flat_owner[:, None] == jnp.arange(groups, dtype=jnp.int32)[None, :]).astype(
        jnp.bfloat16
    )
    position = jnp.arange(count, dtype=jnp.int32)
    earlier = (position[None, :] < position[:, None]).astype(jnp.bfloat16)
    before = jnp.dot(earlier, owner_hits, preferred_element_type=jnp.float32)
    slot = jnp.sum(before * owner_hits.astype(jnp.float32), axis=1).astype(jnp.int32)
    return (flat_owner, slot)


def angle_tables(count, step, lag_count):
    period = 2 * 2048
    lag_value = jnp.arange(lag_count, dtype=jnp.int32) - lag_count // 2
    m = jnp.arange(count, dtype=jnp.int32)
    phase = jnp.mod((m * step)[:, None] * lag_value[None, :], period)
    angle = phase.astype(jnp.float32) * (2.0 * math.pi / period)
    return jnp.cos(angle), jnp.sin(angle)


def build_table(bin_count, lag_count, after):
    hi_step = 64
    hi_count = bin_count // hi_step
    cos_hi, sin_hi = angle_tables(hi_count, hi_step, lag_count)
    cos_lo, sin_lo = angle_tables(hi_step, 1, lag_count)
    cos_hi, sin_hi, cos_lo, sin_lo, _ = lax.optimization_barrier(
        (cos_hi, sin_hi, cos_lo, sin_lo, after)
    )
    frequency = jnp.arange(bin_count, dtype=jnp.int32).reshape(hi_count, hi_step, 1)
    weight = jnp.where(frequency == 0, 1.0, 2.0).astype(jnp.float32)
    cos_full = (cos_hi[:, None, :] * cos_lo[None, :, :] - sin_hi[:, None, :] * sin_lo[None, :, :]) * weight
    sin_full = (sin_hi[:, None, :] * cos_lo[None, :, :] + cos_hi[:, None, :] * sin_lo[None, :, :]) * weight
    cos_part = cos_full.astype(jnp.bfloat16).reshape(bin_count, lag_count)
    sin_part = (-sin_full).astype(jnp.bfloat16).reshape(bin_count, lag_count)
    return cos_part, sin_part


def select_rows(index, block):
    count = block.shape[0]
    chooser = (index[:, None] == jnp.arange(count, dtype=jnp.int32)[None, :]).astype(block.dtype)
    return jnp.dot(chooser, block, preferred_element_type=jnp.float32).astype(block.dtype)


def cross_rows(left_rows, right_rows):
    bin_count = left_rows.shape[-1] // 2
    left_real, left_imag = (left_rows[..., :bin_count], left_rows[..., bin_count:])
    right_real, right_imag = (right_rows[..., :bin_count], right_rows[..., bin_count:])
    real_cross = left_real * right_real + left_imag * right_imag
    imag_cross = left_imag * right_real - left_real * right_imag
    return real_cross.astype(jnp.bfloat16), imag_cross.astype(jnp.bfloat16)


def local(spectra, pair_first, pair_second, pair_owner):
    chips = lax.axis_size("wx")
    cores = lax.axis_size("wc")
    groups = chips * cores
    peers = lax.axis_size("sta")
    bin_count = spectra.shape[-1] // 2
    windows_all = spectra.shape[0] * groups
    factor = 1.0 / math.sqrt(2 * bin_count * windows_all)
    whitened = whiten(spectra[0], SMOOTH_HALF)
    first_rows = pair_first[0]
    second_rows = pair_second[0]
    offsets = first_rows.shape[0]

    z_pairs = [(i, (i - 2) % peers) for i in range(peers)]
    to_even = [(i, i - 1) for i in range(1, peers, 2)]
    to_odd = [(i, i + 1) for i in range(0, peers, 2)]
    rounds = offsets // 2
    chain = [whitened]
    for _ in range(rounds):
        chain.append(shifted(chain[-1], "sta", z_pairs))
    partner_rows = [None] * offsets
    for r in range(rounds + 1):
        partner_rows[2 * r] = select_rows(second_rows[2 * r], chain[r])
    table_after = None
    me = lax.axis_index("sta")
    is_odd = (me % 2) == 1
    last_odd = 2 * rounds - 1
    partner_first, partner_second = shifted(
        (first_rows[last_odd], second_rows[last_odd]), "sta", to_even
    )
    for m in range(rounds):
        from_odd = shifted(chain[m], "sta", to_even)
        if m == 0:
            partner_own = from_odd
        if m + 1 < rounds:
            from_even = shifted(chain[m + 1], "sta", to_odd)
            if m == 1:
                table_after = from_even
            partner_rows[2 * m + 1] = select_rows(second_rows[2 * m + 1], from_odd).astype(
                jnp.float32
            ) + select_rows(second_rows[2 * m + 1], from_even).astype(jnp.float32)
        else:
            partner_rows[2 * m + 1] = select_rows(second_rows[2 * m + 1], from_odd)

    cos_table, sin_table = build_table(bin_count, LAGS, table_after)
    pair_count = first_rows.shape[1]
    own_all = select_rows(first_rows.reshape(-1), whitened)
    pieces = []
    for offset_step in range(offsets):
        own_rows = own_all[offset_step * pair_count : (offset_step + 1) * pair_count]
        pieces.append(
            cross_rows(own_rows.astype(jnp.float32), partner_rows[offset_step].astype(jnp.float32))
        )
    real_value = jnp.concatenate([piece[0] for piece in pieces], axis=0)
    imag_value = jnp.concatenate([piece[1] for piece in pieces], axis=0)
    transformed = (
        (
            jnp.dot(real_value, cos_table, preferred_element_type=jnp.float32)
            + jnp.dot(imag_value, sin_table, preferred_element_type=jnp.float32)
        )
        * factor
    ).astype(jnp.bfloat16)
    transformed = lax.optimization_barrier(transformed)
    help_real, help_imag = cross_rows(
        select_rows(partner_first, partner_own).astype(jnp.float32),
        select_rows(partner_second, chain[rounds]).astype(jnp.float32),
    )
    helped = (
        (
            jnp.dot(help_real, cos_table, preferred_element_type=jnp.float32)
            + jnp.dot(help_imag, sin_table, preferred_element_type=jnp.float32)
        )
        * factor
    ).astype(jnp.bfloat16)
    helped = shifted(helped, "sta", to_odd)
    late_rows = slice(last_odd * pair_count, (last_odd + 1) * pair_count)
    transformed = transformed.at[late_rows].set(
        jnp.where(is_odd, helped, transformed[late_rows])
    )
    pair_rows = real_value.shape[0]
    capacity = 2 * pair_rows // groups
    padded_capacity = -(-capacity // 8) * 8
    owner_row, _ = lax.optimization_barrier((pair_owner[0], chain[2]))
    owners, slot_of = owner_slots(owner_row, groups)
    target = ((owners % cores) * chips + owners // cores) * padded_capacity + slot_of
    placement = (
        target[None, :] == jnp.arange(groups * padded_capacity, dtype=jnp.int32)[:, None]
    ).astype(jnp.bfloat16)
    outgoing = jnp.dot(placement, transformed, preferred_element_type=jnp.float32).astype(
        jnp.bfloat16
    )
    outgoing = outgoing.reshape(cores, chips, padded_capacity, LAGS)
    on_chip = lax.all_to_all(outgoing, "wc", split_axis=0, concat_axis=0, tiled=True)
    chip_sum = jnp.sum(on_chip.astype(jnp.float32), axis=0).astype(jnp.bfloat16)
    received = lax.all_to_all(chip_sum, "wx", split_axis=0, concat_axis=0, tiled=True)
    result = jnp.sum(received.astype(jnp.float32), axis=0).astype(jnp.bfloat16)[:capacity]
    return result[None]


def solution(mesh):
    sta_count, win_count = mesh.devices.shape
    split_mesh = Mesh(mesh.devices.reshape(sta_count, win_count // 2, 2), ("sta", "wx", "wc"))
    win = ("wx", "wc")
    placed = (
        P(win, "sta", None),
        P("sta", None, None),
        P("sta", None, None),
        P("sta", None, None),
    )
    return jax.shard_map(
        local, mesh=split_mesh, in_specs=placed, out_specs=P("sta", win, None), check_vma=False
    )
```

```python
import math

import jax
import jax.numpy as jnp
from jax import lax
from jax.sharding import Mesh, PartitionSpec as P

LAGS = 1024
SMOOTH_HALF = 10


floor_level = 0.5


def shifted(value, axis, pairs):
    return lax.ppermute(value, axis, pairs)


def whiten(spectra, half_width):
    bin_count = spectra.shape[-1] // 2
    real_part = spectra[..., :bin_count].astype(jnp.float32)
    imag_part = spectra[..., bin_count:].astype(jnp.float32)
    amplitude = jnp.sqrt(real_part * real_part + imag_part * imag_part)
    padded = jnp.pad(amplitude, ((0, 0), (half_width, half_width)))
    running = padded[..., 0:bin_count]
    for offset in range(1, 2 * half_width + 1):
        running = running + padded[..., offset : offset + bin_count]
    smooth = running / (2 * half_width + 1)
    inverse = 1.0 / jnp.maximum(smooth, floor_level)
    return jnp.concatenate([real_part * inverse, imag_part * inverse], axis=-1).astype(jnp.bfloat16)


def owner_slots(owners, groups):
    flat_owner = owners.reshape(-1)
    count = flat_owner.shape[0]
    owner_hits = (flat_owner[:, None] == jnp.arange(groups, dtype=jnp.int32)[None, :]).astype(
        jnp.bfloat16
    )
    position = jnp.arange(count, dtype=jnp.int32)
    earlier = (position[None, :] < position[:, None]).astype(jnp.bfloat16)
    before = jnp.dot(earlier, owner_hits, preferred_element_type=jnp.float32)
    slot = jnp.sum(before * owner_hits.astype(jnp.float32), axis=1).astype(jnp.int32)
    return (flat_owner, slot)


def angle_tables(count, step, lag_count):
    period = 2 * 2048
    lag_value = jnp.arange(lag_count, dtype=jnp.int32) - lag_count // 2
    m = jnp.arange(count, dtype=jnp.int32)
    phase = jnp.mod((m * step)[:, None] * lag_value[None, :], period)
    angle = phase.astype(jnp.float32) * (2.0 * math.pi / period)
    return jnp.cos(angle), jnp.sin(angle)


def build_table(bin_count, lag_count, after):
    hi_step = 64
    hi_count = bin_count // hi_step
    cos_hi, sin_hi = angle_tables(hi_count, hi_step, lag_count)
    cos_lo, sin_lo = angle_tables(hi_step, 1, lag_count)
    cos_hi, sin_hi, cos_lo, sin_lo, _ = lax.optimization_barrier(
        (cos_hi, sin_hi, cos_lo, sin_lo, after)
    )
    frequency = jnp.arange(bin_count, dtype=jnp.int32).reshape(hi_count, hi_step, 1)
    weight = jnp.where(frequency == 0, 1.0, 2.0).astype(jnp.float32)
    cos_full = (cos_hi[:, None, :] * cos_lo[None, :, :] - sin_hi[:, None, :] * sin_lo[None, :, :]) * weight
    sin_full = (sin_hi[:, None, :] * cos_lo[None, :, :] + cos_hi[:, None, :] * sin_lo[None, :, :]) * weight
    cos_part = cos_full.astype(jnp.bfloat16).reshape(bin_count, lag_count)
    sin_part = (-sin_full).astype(jnp.bfloat16).reshape(bin_count, lag_count)
    return cos_part, sin_part


def select_rows(index, block):
    count = block.shape[0]
    chooser = (index[:, None] == jnp.arange(count, dtype=jnp.int32)[None, :]).astype(block.dtype)
    return jnp.dot(chooser, block, preferred_element_type=jnp.float32).astype(block.dtype)


def cross_rows(left_rows, right_rows):
    bin_count = left_rows.shape[-1] // 2
    left_real, left_imag = (left_rows[..., :bin_count], left_rows[..., bin_count:])
    right_real, right_imag = (right_rows[..., :bin_count], right_rows[..., bin_count:])
    real_cross = left_real * right_real + left_imag * right_imag
    imag_cross = left_imag * right_real - left_real * right_imag
    return real_cross.astype(jnp.bfloat16), imag_cross.astype(jnp.bfloat16)


def local(spectra, pair_first, pair_second, pair_owner):
    chips = lax.axis_size("wx")
    cores = lax.axis_size("wc")
    groups = chips * cores
    peers = lax.axis_size("sta")
    bin_count = spectra.shape[-1] // 2
    windows_all = spectra.shape[0] * groups
    factor = 1.0 / math.sqrt(2 * bin_count * windows_all)
    whitened = whiten(spectra[0], SMOOTH_HALF)
    first_rows = pair_first[0]
    second_rows = pair_second[0]
    offsets = first_rows.shape[0]

    z_pairs = [(i, (i - 2) % peers) for i in range(peers)]
    to_even = [(i, i - 1) for i in range(1, peers, 2)]
    to_odd = [(i, i + 1) for i in range(0, peers, 2)]
    rounds = offsets // 2
    chain = [whitened]
    for _ in range(rounds):
        chain.append(shifted(chain[-1], "sta", z_pairs))
    partner_rows = [None] * offsets
    for r in range(rounds + 1):
        partner_rows[2 * r] = select_rows(second_rows[2 * r], chain[r])
    table_after = None
    me = lax.axis_index("sta")
    is_odd = (me % 2) == 1
    last_odd = 2 * rounds - 1
    partner_first, partner_second = shifted(
        (first_rows[last_odd], second_rows[last_odd]), "sta", to_even
    )
    for m in range(rounds):
        from_odd = shifted(chain[m], "sta", to_even)
        if m == 0:
            partner_own = from_odd
        if m + 1 < rounds:
            even_block = chain[m + 1]
            if m == 1:
                even_block, _ = lax.optimization_barrier((even_block, chain[m + 2]))
            from_even = shifted(even_block, "sta", to_odd)
            if m == 1:
                table_after = from_even
            partner_rows[2 * m + 1] = select_rows(second_rows[2 * m + 1], from_odd).astype(
                jnp.float32
            ) + select_rows(second_rows[2 * m + 1], from_even).astype(jnp.float32)
        else:
            partner_rows[2 * m + 1] = select_rows(second_rows[2 * m + 1], from_odd)

    cos_table, sin_table = build_table(bin_count, LAGS, table_after)
    pair_count = first_rows.shape[1]
    own_all = select_rows(first_rows.reshape(-1), whitened)
    pieces = []
    for offset_step in range(offsets):
        own_rows = own_all[offset_step * pair_count : (offset_step + 1) * pair_count]
        pieces.append(
            cross_rows(own_rows.astype(jnp.float32), partner_rows[offset_step].astype(jnp.float32))
        )
    real_value = jnp.concatenate([piece[0] for piece in pieces], axis=0)
    imag_value = jnp.concatenate([piece[1] for piece in pieces], axis=0)
    transformed = (
        (
            jnp.dot(real_value, cos_table, preferred_element_type=jnp.float32)
            + jnp.dot(imag_value, sin_table, preferred_element_type=jnp.float32)
        )
        * factor
    ).astype(jnp.bfloat16)
    transformed = lax.optimization_barrier(transformed)
    help_real, help_imag = cross_rows(
        select_rows(partner_first, partner_own).astype(jnp.float32),
        select_rows(partner_second, chain[rounds]).astype(jnp.float32),
    )
    helped = (
        (
            jnp.dot(help_real, cos_table, preferred_element_type=jnp.float32)
            + jnp.dot(help_imag, sin_table, preferred_element_type=jnp.float32)
        )
        * factor
    ).astype(jnp.bfloat16)
    helped = shifted(helped, "sta", to_odd)
    late_rows = slice(last_odd * pair_count, (last_odd + 1) * pair_count)
    transformed = transformed.at[late_rows].set(
        jnp.where(is_odd, helped, transformed[late_rows])
    )
    pair_rows = real_value.shape[0]
    capacity = 2 * pair_rows // groups
    padded_capacity = -(-capacity // 8) * 8
    owner_row, _ = lax.optimization_barrier((pair_owner[0], chain[2]))
    owners, slot_of = owner_slots(owner_row, groups)
    target = ((owners % cores) * chips + owners // cores) * padded_capacity + slot_of
    placement = (
        target[None, :] == jnp.arange(groups * padded_capacity, dtype=jnp.int32)[:, None]
    ).astype(jnp.bfloat16)
    outgoing = jnp.dot(placement, transformed, preferred_element_type=jnp.float32).astype(
        jnp.bfloat16
    )
    outgoing = outgoing.reshape(cores, chips, padded_capacity, LAGS)
    on_chip = lax.all_to_all(outgoing, "wc", split_axis=0, concat_axis=0, tiled=True)
    chip_sum = jnp.sum(on_chip.astype(jnp.float32), axis=0).astype(jnp.bfloat16)
    received = lax.all_to_all(chip_sum, "wx", split_axis=0, concat_axis=0, tiled=True)
    result = jnp.sum(received.astype(jnp.float32), axis=0).astype(jnp.bfloat16)[:capacity]
    return result[None]


def solution(mesh):
    sta_count, win_count = mesh.devices.shape
    split_mesh = Mesh(mesh.devices.reshape(sta_count, win_count // 2, 2), ("sta", "wx", "wc"))
    win = ("wx", "wc")
    placed = (
        P(win, "sta", None),
        P("sta", None, None),
        P("sta", None, None),
        P("sta", None, None),
    )
    return jax.shard_map(
        local, mesh=split_mesh, in_specs=placed, out_specs=P("sta", win, None), check_vma=False
    )
```

```python
import math

import jax
import jax.numpy as jnp
from jax import lax
from jax.sharding import Mesh, PartitionSpec as P

LAGS = 1024
SMOOTH_HALF = 10


floor_level = 0.5


def shifted(value, axis, pairs):
    return lax.ppermute(value, axis, pairs)


def whiten(spectra, half_width):
    bin_count = spectra.shape[-1] // 2
    real_part = spectra[..., :bin_count].astype(jnp.float32)
    imag_part = spectra[..., bin_count:].astype(jnp.float32)
    amplitude = jnp.sqrt(real_part * real_part + imag_part * imag_part)
    padded = jnp.pad(amplitude, ((0, 0), (half_width, half_width)))
    taps = 2 * half_width + 1
    runs = {1: padded}
    width = 1
    while 2 * width <= taps:
        prior = runs[width]
        runs[2 * width] = prior[..., :-width] + prior[..., width:]
        width *= 2
    running = None
    start = 0
    for width in sorted(runs, reverse=True):
        if taps - start >= width:
            piece = runs[width][..., start : start + bin_count]
            running = piece if running is None else running + piece
            start += width
    smooth = running / (2 * half_width + 1)
    inverse = 1.0 / jnp.maximum(smooth, floor_level)
    return jnp.concatenate([real_part * inverse, imag_part * inverse], axis=-1).astype(jnp.bfloat16)


def owner_slots(owners, groups):
    flat_owner = owners.reshape(-1)
    count = flat_owner.shape[0]
    owner_hits = (flat_owner[:, None] == jnp.arange(groups, dtype=jnp.int32)[None, :]).astype(
        jnp.bfloat16
    )
    position = jnp.arange(count, dtype=jnp.int32)
    earlier = (position[None, :] < position[:, None]).astype(jnp.bfloat16)
    before = jnp.dot(earlier, owner_hits, preferred_element_type=jnp.float32)
    slot = jnp.sum(before * owner_hits.astype(jnp.float32), axis=1).astype(jnp.int32)
    return (flat_owner, slot)


def angle_tables(count, step, lag_count):
    period = 2 * 2048
    lag_value = jnp.arange(lag_count, dtype=jnp.int32) - lag_count // 2
    m = jnp.arange(count, dtype=jnp.int32)
    phase = jnp.mod((m * step)[:, None] * lag_value[None, :], period)
    angle = phase.astype(jnp.float32) * (2.0 * math.pi / period)
    return jnp.cos(angle), jnp.sin(angle)


def build_table(bin_count, lag_count, after):
    hi_step = 64
    hi_count = bin_count // hi_step
    cos_hi, sin_hi = angle_tables(hi_count, hi_step, lag_count)
    cos_lo, sin_lo = angle_tables(hi_step, 1, lag_count)
    cos_hi, sin_hi, cos_lo, sin_lo, _ = lax.optimization_barrier(
        (cos_hi, sin_hi, cos_lo, sin_lo, after)
    )
    frequency = jnp.arange(bin_count, dtype=jnp.int32).reshape(hi_count, hi_step, 1)
    weight = jnp.where(frequency == 0, 1.0, 2.0).astype(jnp.float32)
    cos_full = (cos_hi[:, None, :] * cos_lo[None, :, :] - sin_hi[:, None, :] * sin_lo[None, :, :]) * weight
    sin_full = (sin_hi[:, None, :] * cos_lo[None, :, :] + cos_hi[:, None, :] * sin_lo[None, :, :]) * weight
    cos_part = cos_full.astype(jnp.bfloat16).reshape(bin_count, lag_count)
    sin_part = (-sin_full).astype(jnp.bfloat16).reshape(bin_count, lag_count)
    return cos_part, sin_part


def select_rows(index, block):
    count = block.shape[0]
    chooser = (index[:, None] == jnp.arange(count, dtype=jnp.int32)[None, :]).astype(block.dtype)
    return jnp.dot(chooser, block, preferred_element_type=jnp.float32).astype(block.dtype)


def cross_rows(left_rows, right_rows):
    bin_count = left_rows.shape[-1] // 2
    left_real, left_imag = (left_rows[..., :bin_count], left_rows[..., bin_count:])
    right_real, right_imag = (right_rows[..., :bin_count], right_rows[..., bin_count:])
    real_cross = left_real * right_real + left_imag * right_imag
    imag_cross = left_imag * right_real - left_real * right_imag
    return real_cross.astype(jnp.bfloat16), imag_cross.astype(jnp.bfloat16)


def local(spectra, pair_first, pair_second, pair_owner):
    chips = lax.axis_size("wx")
    cores = lax.axis_size("wc")
    groups = chips * cores
    peers = lax.axis_size("sta")
    bin_count = spectra.shape[-1] // 2
    windows_all = spectra.shape[0] * groups
    factor = 1.0 / math.sqrt(2 * bin_count * windows_all)
    whitened = whiten(spectra[0], SMOOTH_HALF)
    first_rows = pair_first[0]
    second_rows = pair_second[0]
    offsets = first_rows.shape[0]

    z_pairs = [(i, (i - 2) % peers) for i in range(peers)]
    to_even = [(i, i - 1) for i in range(1, peers, 2)]
    to_odd = [(i, i + 1) for i in range(0, peers, 2)]
    rounds = offsets // 2
    chain = [whitened]
    for _ in range(rounds):
        chain.append(shifted(chain[-1], "sta", z_pairs))
    partner_rows = [None] * offsets
    for r in range(rounds + 1):
        partner_rows[2 * r] = select_rows(second_rows[2 * r], chain[r])
    table_after = None
    me = lax.axis_index("sta")
    is_odd = (me % 2) == 1
    last_odd = 2 * rounds - 1
    partner_first, partner_second = shifted(
        (first_rows[last_odd], second_rows[last_odd]), "sta", to_even
    )
    for m in range(rounds):
        from_odd = shifted(chain[m], "sta", to_even)
        if m == 0:
            partner_own = from_odd
        if m + 1 < rounds:
            from_even = shifted(chain[m + 1], "sta", to_odd)
            if m == 1:
                table_after = from_even
            partner_rows[2 * m + 1] = select_rows(second_rows[2 * m + 1], from_odd).astype(
                jnp.float32
            ) + select_rows(second_rows[2 * m + 1], from_even).astype(jnp.float32)
        else:
            partner_rows[2 * m + 1] = select_rows(second_rows[2 * m + 1], from_odd)

    cos_table, sin_table = build_table(bin_count, LAGS, table_after)
    pair_count = first_rows.shape[1]
    own_all = select_rows(first_rows.reshape(-1), whitened)
    pieces = []
    for offset_step in range(offsets):
        own_rows = own_all[offset_step * pair_count : (offset_step + 1) * pair_count]
        pieces.append(
            cross_rows(own_rows.astype(jnp.float32), partner_rows[offset_step].astype(jnp.float32))
        )
    real_value = jnp.concatenate([piece[0] for piece in pieces], axis=0)
    imag_value = jnp.concatenate([piece[1] for piece in pieces], axis=0)
    transformed = (
        (
            jnp.dot(real_value, cos_table, preferred_element_type=jnp.float32)
            + jnp.dot(imag_value, sin_table, preferred_element_type=jnp.float32)
        )
        * factor
    ).astype(jnp.bfloat16)
    transformed = lax.optimization_barrier(transformed)
    help_real, help_imag = cross_rows(
        select_rows(partner_first, partner_own).astype(jnp.float32),
        select_rows(partner_second, chain[rounds]).astype(jnp.float32),
    )
    helped = (
        (
            jnp.dot(help_real, cos_table, preferred_element_type=jnp.float32)
            + jnp.dot(help_imag, sin_table, preferred_element_type=jnp.float32)
        )
        * factor
    ).astype(jnp.bfloat16)
    helped = shifted(helped, "sta", to_odd)
    late_rows = slice(last_odd * pair_count, (last_odd + 1) * pair_count)
    transformed = transformed.at[late_rows].set(
        jnp.where(is_odd, helped, transformed[late_rows])
    )
    pair_rows = real_value.shape[0]
    capacity = 2 * pair_rows // groups
    padded_capacity = -(-capacity // 8) * 8
    owner_row, _ = lax.optimization_barrier((pair_owner[0], chain[2]))
    owners, slot_of = owner_slots(owner_row, groups)
    target = ((owners % cores) * chips + owners // cores) * padded_capacity + slot_of
    placement = (
        target[None, :] == jnp.arange(groups * padded_capacity, dtype=jnp.int32)[:, None]
    ).astype(jnp.bfloat16)
    outgoing = jnp.dot(placement, transformed, preferred_element_type=jnp.float32).astype(
        jnp.bfloat16
    )
    outgoing = outgoing.reshape(cores, chips, padded_capacity, LAGS)
    on_chip = lax.all_to_all(outgoing, "wc", split_axis=0, concat_axis=0, tiled=True)
    chip_sum = jnp.sum(on_chip.astype(jnp.float32), axis=0).astype(jnp.bfloat16)
    received = lax.all_to_all(chip_sum, "wx", split_axis=0, concat_axis=0, tiled=True)
    result = jnp.sum(received.astype(jnp.float32), axis=0).astype(jnp.bfloat16)[:capacity]
    return result[None]


def solution(mesh):
    sta_count, win_count = mesh.devices.shape
    split_mesh = Mesh(mesh.devices.reshape(sta_count, win_count // 2, 2), ("sta", "wx", "wc"))
    win = ("wx", "wc")
    placed = (
        P(win, "sta", None),
        P("sta", None, None),
        P("sta", None, None),
        P("sta", None, None),
    )
    return jax.shard_map(
        local, mesh=split_mesh, in_specs=placed, out_specs=P("sta", win, None), check_vma=False
    )
```

```python
import math

import jax
import jax.numpy as jnp
from jax import lax
from jax.sharding import Mesh, PartitionSpec as P

LAGS = 1024
SMOOTH_HALF = 10


floor_level = 0.5


def shifted(value, axis, pairs):
    return lax.ppermute(value, axis, pairs)


def whiten(spectra, half_width):
    bin_count = spectra.shape[-1] // 2
    real_part = spectra[..., :bin_count].astype(jnp.float32)
    imag_part = spectra[..., bin_count:].astype(jnp.float32)
    amplitude = jnp.sqrt(real_part * real_part + imag_part * imag_part)
    padded = jnp.pad(amplitude, ((0, 0), (half_width, half_width)))
    taps = 2 * half_width + 1
    runs = {1: padded}
    width = 1
    while 2 * width <= taps:
        prior = runs[width]
        runs[2 * width] = prior[..., :-width] + prior[..., width:]
        width *= 2
    running = None
    start = 0
    for width in sorted(runs, reverse=True):
        if taps - start >= width:
            piece = runs[width][..., start : start + bin_count]
            running = piece if running is None else running + piece
            start += width
    smooth = running / (2 * half_width + 1)
    inverse = 1.0 / jnp.maximum(smooth, floor_level)
    return jnp.concatenate([real_part * inverse, imag_part * inverse], axis=-1).astype(jnp.bfloat16)


def owner_slots(owners, groups):
    flat_owner = owners.reshape(-1)
    count = flat_owner.shape[0]
    owner_hits = (flat_owner[:, None] == jnp.arange(groups, dtype=jnp.int32)[None, :]).astype(
        jnp.bfloat16
    )
    position = jnp.arange(count, dtype=jnp.int32)
    earlier = (position[None, :] < position[:, None]).astype(jnp.bfloat16)
    before = jnp.dot(earlier, owner_hits, preferred_element_type=jnp.float32)
    slot = jnp.sum(before * owner_hits.astype(jnp.float32), axis=1).astype(jnp.int32)
    return (flat_owner, slot)


def angle_tables(count, step, lag_count):
    period = 2 * 2048
    lag_value = jnp.arange(lag_count, dtype=jnp.int32) - lag_count // 2
    m = jnp.arange(count, dtype=jnp.int32)
    phase = jnp.mod((m * step)[:, None] * lag_value[None, :], period)
    angle = phase.astype(jnp.float32) * (2.0 * math.pi / period)
    return jnp.cos(angle), jnp.sin(angle)


def build_table(bin_count, lag_count, after):
    hi_step = 64
    hi_count = bin_count // hi_step
    cos_hi, sin_hi = angle_tables(hi_count, hi_step, lag_count)
    cos_lo, sin_lo = angle_tables(hi_step, 1, lag_count)
    cos_hi, sin_hi, cos_lo, sin_lo, _ = lax.optimization_barrier(
        (cos_hi, sin_hi, cos_lo, sin_lo, after)
    )
    frequency = jnp.arange(bin_count, dtype=jnp.int32).reshape(hi_count, hi_step, 1)
    weight = jnp.where(frequency == 0, 1.0, 2.0).astype(jnp.float32)
    cos_full = (cos_hi[:, None, :] * cos_lo[None, :, :] - sin_hi[:, None, :] * sin_lo[None, :, :]) * weight
    sin_full = (sin_hi[:, None, :] * cos_lo[None, :, :] + cos_hi[:, None, :] * sin_lo[None, :, :]) * weight
    cos_part = cos_full.astype(jnp.bfloat16).reshape(bin_count, lag_count)
    sin_part = (-sin_full).astype(jnp.bfloat16).reshape(bin_count, lag_count)
    return cos_part, sin_part


def select_rows(index, block):
    count = block.shape[0]
    chooser = (index[:, None] == jnp.arange(count, dtype=jnp.int32)[None, :]).astype(block.dtype)
    return jnp.dot(chooser, block, preferred_element_type=jnp.float32).astype(block.dtype)


def cross_rows(left_rows, right_rows):
    bin_count = left_rows.shape[-1] // 2
    left_real, left_imag = (left_rows[..., :bin_count], left_rows[..., bin_count:])
    right_real, right_imag = (right_rows[..., :bin_count], right_rows[..., bin_count:])
    real_cross = left_real * right_real + left_imag * right_imag
    imag_cross = left_imag * right_real - left_real * right_imag
    return real_cross.astype(jnp.bfloat16), imag_cross.astype(jnp.bfloat16)


def local(spectra, pair_first, pair_second, pair_owner):
    chips = lax.axis_size("wx")
    cores = lax.axis_size("wc")
    groups = chips * cores
    peers = lax.axis_size("sta")
    bin_count = spectra.shape[-1] // 2
    windows_all = spectra.shape[0] * groups
    factor = 1.0 / math.sqrt(2 * bin_count * windows_all)
    whitened = whiten(spectra[0], SMOOTH_HALF)
    first_rows = pair_first[0]
    second_rows = pair_second[0]
    offsets = first_rows.shape[0]

    z_pairs = [(i, (i - 2) % peers) for i in range(peers)]
    to_even = [(i, i - 1) for i in range(1, peers, 2)]
    to_odd = [(i, i + 1) for i in range(0, peers, 2)]
    rounds = offsets // 2
    chain = [whitened]
    for _ in range(rounds):
        chain.append(shifted(chain[-1], "sta", z_pairs))
    partner_rows = [None] * offsets
    for r in range(rounds + 1):
        partner_rows[2 * r] = select_rows(second_rows[2 * r], chain[r])
    table_after = None
    me = lax.axis_index("sta")
    is_odd = (me % 2) == 1
    last_odd = 2 * rounds - 1
    partner_index = shifted(
        jnp.stack([first_rows[last_odd], second_rows[last_odd]]), "sta", to_even
    )
    partner_first, partner_second = partner_index[0], partner_index[1]
    for m in range(rounds):
        from_odd = shifted(chain[m], "sta", to_even)
        if m == 0:
            partner_own = from_odd
        if m + 1 < rounds:
            from_even = shifted(chain[m + 1], "sta", to_odd)
            if m == 1:
                table_after = from_even
            partner_rows[2 * m + 1] = select_rows(second_rows[2 * m + 1], from_odd).astype(
                jnp.float32
            ) + select_rows(second_rows[2 * m + 1], from_even).astype(jnp.float32)
        else:
            partner_rows[2 * m + 1] = select_rows(second_rows[2 * m + 1], from_odd)

    cos_table, sin_table = build_table(bin_count, LAGS, table_after)
    pair_count = first_rows.shape[1]
    own_all = select_rows(first_rows.reshape(-1), whitened)
    pieces = []
    for offset_step in range(offsets):
        own_rows = own_all[offset_step * pair_count : (offset_step + 1) * pair_count]
        pieces.append(
            cross_rows(own_rows.astype(jnp.float32), partner_rows[offset_step].astype(jnp.float32))
        )
    real_value = jnp.concatenate([piece[0] for piece in pieces], axis=0)
    imag_value = jnp.concatenate([piece[1] for piece in pieces], axis=0)
    transformed = (
        (
            jnp.dot(real_value, cos_table, preferred_element_type=jnp.float32)
            + jnp.dot(imag_value, sin_table, preferred_element_type=jnp.float32)
        )
        * factor
    ).astype(jnp.bfloat16)
    transformed = lax.optimization_barrier(transformed)
    help_real, help_imag = cross_rows(
        select_rows(partner_first, partner_own).astype(jnp.float32),
        select_rows(partner_second, chain[rounds]).astype(jnp.float32),
    )
    helped = (
        (
            jnp.dot(help_real, cos_table, preferred_element_type=jnp.float32)
            + jnp.dot(help_imag, sin_table, preferred_element_type=jnp.float32)
        )
        * factor
    ).astype(jnp.bfloat16)
    helped = shifted(helped, "sta", to_odd)
    late_rows = slice(last_odd * pair_count, (last_odd + 1) * pair_count)
    transformed = transformed.at[late_rows].set(
        jnp.where(is_odd, helped, transformed[late_rows])
    )
    pair_rows = real_value.shape[0]
    capacity = 2 * pair_rows // groups
    padded_capacity = -(-capacity // 8) * 8
    owner_row, _ = lax.optimization_barrier((pair_owner[0], chain[2]))
    owners, slot_of = owner_slots(owner_row, groups)
    target = ((owners % cores) * chips + owners // cores) * padded_capacity + slot_of
    placement = (
        target[None, :] == jnp.arange(groups * padded_capacity, dtype=jnp.int32)[:, None]
    ).astype(jnp.bfloat16)
    outgoing = jnp.dot(placement, transformed, preferred_element_type=jnp.float32).astype(
        jnp.bfloat16
    )
    outgoing = outgoing.reshape(cores, chips, padded_capacity, LAGS)
    on_chip = lax.all_to_all(outgoing, "wc", split_axis=0, concat_axis=0, tiled=True)
    chip_sum = jnp.sum(on_chip.astype(jnp.float32), axis=0).astype(jnp.bfloat16)
    received = lax.all_to_all(chip_sum, "wx", split_axis=0, concat_axis=0, tiled=True)
    result = jnp.sum(received.astype(jnp.float32), axis=0).astype(jnp.bfloat16)[:capacity]
    return result[None]


def solution(mesh):
    sta_count, win_count = mesh.devices.shape
    split_mesh = Mesh(mesh.devices.reshape(sta_count, win_count // 2, 2), ("sta", "wx", "wc"))
    win = ("wx", "wc")
    placed = (
        P(win, "sta", None),
        P("sta", None, None),
        P("sta", None, None),
        P("sta", None, None),
    )
    return jax.shard_map(
        local, mesh=split_mesh, in_specs=placed, out_specs=P("sta", win, None), check_vma=False
    )
```

```python
import math

import jax
import jax.numpy as jnp
from jax import lax
from jax.sharding import Mesh, PartitionSpec as P

LAGS = 1024
SMOOTH_HALF = 10


floor_level = 0.5


def shifted(value, axis, pairs):
    return lax.ppermute(value, axis, pairs)


def whiten(spectra, half_width):
    bin_count = spectra.shape[-1] // 2
    real_part = spectra[..., :bin_count].astype(jnp.float32)
    imag_part = spectra[..., bin_count:].astype(jnp.float32)
    amplitude = jnp.sqrt(real_part * real_part + imag_part * imag_part)
    padded = jnp.pad(amplitude, ((0, 0), (half_width, half_width)))
    taps = 2 * half_width + 1
    runs = {1: padded}
    width = 1
    while 2 * width <= taps:
        prior = runs[width]
        runs[2 * width] = prior[..., :-width] + prior[..., width:]
        width *= 2
    running = None
    start = 0
    for width in sorted(runs, reverse=True):
        if taps - start >= width:
            piece = runs[width][..., start : start + bin_count]
            running = piece if running is None else running + piece
            start += width
    smooth = running / (2 * half_width + 1)
    inverse = 1.0 / jnp.maximum(smooth, floor_level)
    return jnp.concatenate([real_part * inverse, imag_part * inverse], axis=-1).astype(jnp.bfloat16)


def owner_slots(owners, groups):
    flat_owner = owners.reshape(-1)
    count = flat_owner.shape[0]
    owner_hits = (flat_owner[:, None] == jnp.arange(groups, dtype=jnp.int32)[None, :]).astype(
        jnp.bfloat16
    )
    position = jnp.arange(count, dtype=jnp.int32)
    earlier = (position[None, :] < position[:, None]).astype(jnp.bfloat16)
    before = jnp.dot(earlier, owner_hits, preferred_element_type=jnp.float32)
    slot = jnp.sum(before * owner_hits.astype(jnp.float32), axis=1).astype(jnp.int32)
    return (flat_owner, slot)


def angle_tables(count, step, lag_count):
    period = 2 * 2048
    lag_value = jnp.arange(lag_count, dtype=jnp.int32) - lag_count // 2
    m = jnp.arange(count, dtype=jnp.int32)
    phase = jnp.mod((m * step)[:, None] * lag_value[None, :], period)
    angle = phase.astype(jnp.float32) * (2.0 * math.pi / period)
    return jnp.cos(angle), jnp.sin(angle)


def build_table(bin_count, lag_count, after):
    hi_step = 64
    hi_count = bin_count // hi_step
    cos_hi, sin_hi = angle_tables(hi_count, hi_step, lag_count)
    cos_lo, sin_lo = angle_tables(hi_step, 1, lag_count)
    cos_hi, sin_hi, cos_lo, sin_lo, _ = lax.optimization_barrier(
        (cos_hi, sin_hi, cos_lo, sin_lo, after)
    )
    frequency = jnp.arange(bin_count, dtype=jnp.int32).reshape(hi_count, hi_step, 1)
    weight = jnp.where(frequency == 0, 1.0, 2.0).astype(jnp.float32)
    cos_full = (cos_hi[:, None, :] * cos_lo[None, :, :] - sin_hi[:, None, :] * sin_lo[None, :, :]) * weight
    sin_full = (sin_hi[:, None, :] * cos_lo[None, :, :] + cos_hi[:, None, :] * sin_lo[None, :, :]) * weight
    cos_part = cos_full.astype(jnp.bfloat16).reshape(bin_count, lag_count)
    sin_part = (-sin_full).astype(jnp.bfloat16).reshape(bin_count, lag_count)
    return cos_part, sin_part


def select_rows(index, block):
    count = block.shape[0]
    chooser = (index[:, None] == jnp.arange(count, dtype=jnp.int32)[None, :]).astype(block.dtype)
    return jnp.dot(chooser, block, preferred_element_type=jnp.float32).astype(block.dtype)


def cross_rows(left_rows, right_rows):
    bin_count = left_rows.shape[-1] // 2
    left_real, left_imag = (left_rows[..., :bin_count], left_rows[..., bin_count:])
    right_real, right_imag = (right_rows[..., :bin_count], right_rows[..., bin_count:])
    real_cross = left_real * right_real + left_imag * right_imag
    imag_cross = left_imag * right_real - left_real * right_imag
    return real_cross.astype(jnp.bfloat16), imag_cross.astype(jnp.bfloat16)


def local(spectra, pair_first, pair_second, pair_owner):
    chips = lax.axis_size("wx")
    cores = lax.axis_size("wc")
    groups = chips * cores
    peers = lax.axis_size("sta")
    bin_count = spectra.shape[-1] // 2
    windows_all = spectra.shape[0] * groups
    factor = 1.0 / math.sqrt(2 * bin_count * windows_all)
    whitened = whiten(spectra[0], SMOOTH_HALF)
    first_rows = pair_first[0]
    second_rows = pair_second[0]
    offsets = first_rows.shape[0]

    z_pairs = [(i, (i - 2) % peers) for i in range(peers)]
    to_even = [(i, i - 1) for i in range(1, peers, 2)]
    to_odd = [(i, i + 1) for i in range(0, peers, 2)]
    rounds = offsets // 2
    chain = [whitened]
    for _ in range(rounds):
        chain.append(shifted(chain[-1], "sta", z_pairs))
    partner_rows = [None] * offsets
    for r in range(rounds + 1):
        partner_rows[2 * r] = select_rows(second_rows[2 * r], chain[r])
    table_after = None
    me = lax.axis_index("sta")
    is_odd = (me % 2) == 1
    last_odd = 2 * rounds - 1
    index_slab = jnp.zeros((16, whitened.shape[1]), jnp.bfloat16)
    index_slab = index_slab.at[0, : first_rows.shape[1]].set(first_rows[last_odd].astype(jnp.bfloat16))
    index_slab = index_slab.at[1, : second_rows.shape[1]].set(second_rows[last_odd].astype(jnp.bfloat16))
    block_rows = whitened.shape[0]
    for m in range(rounds):
        if m == 0:
            carried = shifted(jnp.concatenate([chain[0], index_slab], axis=0), "sta", to_even)
            from_odd = carried[:block_rows]
            partner_own = from_odd
            pair_count = first_rows.shape[1]
            partner_first = carried[block_rows, :pair_count].astype(jnp.int32)
            partner_second = carried[block_rows + 1, :pair_count].astype(jnp.int32)
        else:
            from_odd = shifted(chain[m], "sta", to_even)
        if m + 1 < rounds:
            from_even = shifted(chain[m + 1], "sta", to_odd)
            if m == 1:
                table_after = from_even
            partner_rows[2 * m + 1] = select_rows(second_rows[2 * m + 1], from_odd).astype(
                jnp.float32
            ) + select_rows(second_rows[2 * m + 1], from_even).astype(jnp.float32)
        else:
            partner_rows[2 * m + 1] = select_rows(second_rows[2 * m + 1], from_odd)

    cos_table, sin_table = build_table(bin_count, LAGS, table_after)
    pair_count = first_rows.shape[1]
    own_all = select_rows(first_rows.reshape(-1), whitened)
    pieces = []
    for offset_step in range(offsets):
        own_rows = own_all[offset_step * pair_count : (offset_step + 1) * pair_count]
        pieces.append(
            cross_rows(own_rows.astype(jnp.float32), partner_rows[offset_step].astype(jnp.float32))
        )
    real_value = jnp.concatenate([piece[0] for piece in pieces], axis=0)
    imag_value = jnp.concatenate([piece[1] for piece in pieces], axis=0)
    transformed = (
        (
            jnp.dot(real_value, cos_table, preferred_element_type=jnp.float32)
            + jnp.dot(imag_value, sin_table, preferred_element_type=jnp.float32)
        )
        * factor
    ).astype(jnp.bfloat16)
    transformed = lax.optimization_barrier(transformed)
    help_real, help_imag = cross_rows(
        select_rows(partner_first, partner_own).astype(jnp.float32),
        select_rows(partner_second, chain[rounds]).astype(jnp.float32),
    )
    helped = (
        (
            jnp.dot(help_real, cos_table, preferred_element_type=jnp.float32)
            + jnp.dot(help_imag, sin_table, preferred_element_type=jnp.float32)
        )
        * factor
    ).astype(jnp.bfloat16)
    helped = shifted(helped, "sta", to_odd)
    late_rows = slice(last_odd * pair_count, (last_odd + 1) * pair_count)
    transformed = transformed.at[late_rows].set(
        jnp.where(is_odd, helped, transformed[late_rows])
    )
    pair_rows = real_value.shape[0]
    capacity = 2 * pair_rows // groups
    padded_capacity = -(-capacity // 8) * 8
    owner_row, _ = lax.optimization_barrier((pair_owner[0], chain[2]))
    owners, slot_of = owner_slots(owner_row, groups)
    target = ((owners % cores) * chips + owners // cores) * padded_capacity + slot_of
    placement = (
        target[None, :] == jnp.arange(groups * padded_capacity, dtype=jnp.int32)[:, None]
    ).astype(jnp.bfloat16)
    outgoing = jnp.dot(placement, transformed, preferred_element_type=jnp.float32).astype(
        jnp.bfloat16
    )
    outgoing = outgoing.reshape(cores, chips, padded_capacity, LAGS)
    on_chip = lax.all_to_all(outgoing, "wc", split_axis=0, concat_axis=0, tiled=True)
    chip_sum = jnp.sum(on_chip.astype(jnp.float32), axis=0).astype(jnp.bfloat16)
    received = lax.all_to_all(chip_sum, "wx", split_axis=0, concat_axis=0, tiled=True)
    result = jnp.sum(received.astype(jnp.float32), axis=0).astype(jnp.bfloat16)[:capacity]
    return result[None]


def solution(mesh):
    sta_count, win_count = mesh.devices.shape
    split_mesh = Mesh(mesh.devices.reshape(sta_count, win_count // 2, 2), ("sta", "wx", "wc"))
    win = ("wx", "wc")
    placed = (
        P(win, "sta", None),
        P("sta", None, None),
        P("sta", None, None),
        P("sta", None, None),
    )
    return jax.shard_map(
        local, mesh=split_mesh, in_specs=placed, out_specs=P("sta", win, None), check_vma=False
    )
```

```python
import math

import jax
import jax.numpy as jnp
from jax import lax
from jax.sharding import Mesh, PartitionSpec as P

LAGS = 1024
SMOOTH_HALF = 10


floor_level = 0.5


def shifted(value, axis, pairs):
    return lax.ppermute(value, axis, pairs)


def whiten(spectra, half_width):
    bin_count = spectra.shape[-1] // 2
    real_part = spectra[..., :bin_count].astype(jnp.float32)
    imag_part = spectra[..., bin_count:].astype(jnp.float32)
    amplitude = jnp.sqrt(real_part * real_part + imag_part * imag_part)
    padded = jnp.pad(amplitude, ((0, 0), (half_width, half_width)))
    taps = 2 * half_width + 1
    runs = {1: padded}
    width = 1
    while 2 * width <= taps:
        prior = runs[width]
        runs[2 * width] = prior[..., :-width] + prior[..., width:]
        width *= 2
    running = None
    start = 0
    for width in sorted(runs, reverse=True):
        if taps - start >= width:
            piece = runs[width][..., start : start + bin_count]
            running = piece if running is None else running + piece
            start += width
    smooth = running / (2 * half_width + 1)
    inverse = 1.0 / jnp.maximum(smooth, floor_level)
    return jnp.concatenate([real_part * inverse, imag_part * inverse], axis=-1).astype(jnp.bfloat16)


def owner_slots(owners, groups):
    flat_owner = owners.reshape(-1)
    count = flat_owner.shape[0]
    owner_hits = (flat_owner[:, None] == jnp.arange(groups, dtype=jnp.int32)[None, :]).astype(
        jnp.bfloat16
    )
    position = jnp.arange(count, dtype=jnp.int32)
    earlier = (position[None, :] < position[:, None]).astype(jnp.bfloat16)
    before = jnp.dot(earlier, owner_hits, preferred_element_type=jnp.float32)
    slot = jnp.sum(before * owner_hits.astype(jnp.float32), axis=1).astype(jnp.int32)
    return (flat_owner, slot)


def angle_tables(count, step, lag_count):
    period = 2 * 2048
    lag_value = jnp.arange(lag_count, dtype=jnp.int32) - lag_count // 2
    m = jnp.arange(count, dtype=jnp.int32)
    phase = jnp.mod((m * step)[:, None] * lag_value[None, :], period)
    angle = phase.astype(jnp.float32) * (2.0 * math.pi / period)
    return jnp.cos(angle), jnp.sin(angle)


def build_table(bin_count, lag_count, after):
    hi_step = 64
    hi_count = bin_count // hi_step
    cos_hi, sin_hi = angle_tables(hi_count, hi_step, lag_count)
    cos_lo, sin_lo = angle_tables(hi_step, 1, lag_count)
    cos_hi, sin_hi, cos_lo, sin_lo, _ = lax.optimization_barrier(
        (cos_hi, sin_hi, cos_lo, sin_lo, after)
    )
    frequency = jnp.arange(bin_count, dtype=jnp.int32).reshape(hi_count, hi_step, 1)
    weight = jnp.where(frequency == 0, 1.0, 2.0).astype(jnp.float32)
    cos_full = (cos_hi[:, None, :] * cos_lo[None, :, :] - sin_hi[:, None, :] * sin_lo[None, :, :]) * weight
    sin_full = (sin_hi[:, None, :] * cos_lo[None, :, :] + cos_hi[:, None, :] * sin_lo[None, :, :]) * weight
    cos_part = cos_full.astype(jnp.bfloat16).reshape(bin_count, lag_count)
    sin_part = (-sin_full).astype(jnp.bfloat16).reshape(bin_count, lag_count)
    return cos_part, sin_part


def select_rows(index, block):
    count = block.shape[0]
    chooser = (index[:, None] == jnp.arange(count, dtype=jnp.int32)[None, :]).astype(block.dtype)
    return jnp.dot(chooser, block, preferred_element_type=jnp.float32).astype(block.dtype)


def cross_rows(left_rows, right_rows):
    bin_count = left_rows.shape[-1] // 2
    left_real, left_imag = (left_rows[..., :bin_count], left_rows[..., bin_count:])
    right_real, right_imag = (right_rows[..., :bin_count], right_rows[..., bin_count:])
    real_cross = left_real * right_real + left_imag * right_imag
    imag_cross = left_imag * right_real - left_real * right_imag
    return real_cross.astype(jnp.bfloat16), imag_cross.astype(jnp.bfloat16)


def local(spectra, pair_first, pair_second, pair_owner):
    chips = lax.axis_size("wx")
    cores = lax.axis_size("wc")
    groups = chips * cores
    peers = lax.axis_size("sta")
    bin_count = spectra.shape[-1] // 2
    windows_all = spectra.shape[0] * groups
    factor = 1.0 / math.sqrt(2 * bin_count * windows_all)
    whitened = whiten(spectra[0], SMOOTH_HALF)
    first_rows = pair_first[0]
    second_rows = pair_second[0]
    offsets = first_rows.shape[0]

    z_pairs = [(i, (i - 2) % peers) for i in range(peers)]
    to_even = [(i, i - 1) for i in range(1, peers, 2)]
    to_odd = [(i, i + 1) for i in range(0, peers, 2)]
    rounds = offsets // 2
    chain = [whitened]
    for _ in range(rounds):
        chain.append(shifted(chain[-1], "sta", z_pairs))
    partner_rows = [None] * offsets
    for r in range(rounds + 1):
        partner_rows[2 * r] = select_rows(second_rows[2 * r], chain[r])
    table_after = None
    me = lax.axis_index("sta")
    is_odd = (me % 2) == 1
    last_odd = 2 * rounds - 1
    partner_index = shifted(
        jnp.stack([first_rows[last_odd], second_rows[last_odd]]), "sta", to_even
    )
    partner_first, partner_second = partner_index[0], partner_index[1]
    for m in range(rounds):
        from_odd = shifted(chain[m], "sta", to_even)
        if m == 0:
            partner_own = from_odd
        if m + 1 < rounds:
            from_even = shifted(chain[m + 1], "sta", to_odd)
            if m == 1:
                table_after = from_even
            partner_rows[2 * m + 1] = select_rows(second_rows[2 * m + 1], from_odd).astype(
                jnp.float32
            ) + select_rows(second_rows[2 * m + 1], from_even).astype(jnp.float32)
        else:
            partner_rows[2 * m + 1] = select_rows(second_rows[2 * m + 1], from_odd)

    cos_table, sin_table = build_table(bin_count, LAGS, table_after)
    pair_count = first_rows.shape[1]
    own_all = select_rows(first_rows.reshape(-1), whitened)
    pieces = []
    for offset_step in range(offsets):
        own_rows = own_all[offset_step * pair_count : (offset_step + 1) * pair_count]
        pieces.append(
            cross_rows(own_rows.astype(jnp.float32), partner_rows[offset_step].astype(jnp.float32))
        )
    real_value = jnp.concatenate([piece[0] for piece in pieces], axis=0)
    imag_value = jnp.concatenate([piece[1] for piece in pieces], axis=0)
    transformed = (
        (
            jnp.dot(real_value, cos_table, preferred_element_type=jnp.float32)
            + jnp.dot(imag_value, sin_table, preferred_element_type=jnp.float32)
        )
        * factor
    ).astype(jnp.bfloat16)
    transformed = lax.optimization_barrier(transformed)
    help_real, help_imag = cross_rows(
        select_rows(partner_first, partner_own).astype(jnp.float32),
        select_rows(partner_second, chain[rounds]).astype(jnp.float32),
    )
    helped = (
        (
            jnp.dot(help_real, cos_table, preferred_element_type=jnp.float32)
            + jnp.dot(help_imag, sin_table, preferred_element_type=jnp.float32)
        )
        * factor
    ).astype(jnp.bfloat16)
    helped = shifted(helped, "sta", to_odd)
    late_rows = slice(last_odd * pair_count, (last_odd + 1) * pair_count)
    transformed = transformed.at[late_rows].set(
        jnp.where(is_odd, helped, transformed[late_rows])
    )
    pair_rows = real_value.shape[0]
    capacity = 2 * pair_rows // groups
    padded_capacity = -(-capacity // 8) * 8
    owner_row, _ = lax.optimization_barrier((pair_owner[0], chain[2]))
    owners, slot_of = owner_slots(owner_row, groups)
    my_core = lax.axis_index("wc")
    local_row = (owners // cores) * padded_capacity + slot_of
    slot_index = jnp.arange(chips * padded_capacity, dtype=jnp.int32)[:, None]
    own_target = jnp.where(owners % cores == my_core, local_row, -1)
    other_target = jnp.where(owners % cores == my_core, -1, local_row)

    def placed(row_target):
        chooser = (row_target[None, :] == slot_index).astype(jnp.bfloat16)
        return jnp.dot(chooser, transformed, preferred_element_type=jnp.float32).astype(
            jnp.bfloat16
        )

    from_other_core = lax.ppermute(placed(other_target), "wc", [(0, 1), (1, 0)])
    chip_sum = (placed(own_target).astype(jnp.float32) + from_other_core.astype(jnp.float32))
    chip_sum = chip_sum.astype(jnp.bfloat16).reshape(chips, padded_capacity, LAGS)
    received = lax.all_to_all(chip_sum, "wx", split_axis=0, concat_axis=0, tiled=True)
    result = jnp.sum(received.astype(jnp.float32), axis=0).astype(jnp.bfloat16)[:capacity]
    return result[None]


def solution(mesh):
    sta_count, win_count = mesh.devices.shape
    split_mesh = Mesh(mesh.devices.reshape(sta_count, win_count // 2, 2), ("sta", "wx", "wc"))
    win = ("wx", "wc")
    placed = (
        P(win, "sta", None),
        P("sta", None, None),
        P("sta", None, None),
        P("sta", None, None),
    )
    return jax.shard_map(
        local, mesh=split_mesh, in_specs=placed, out_specs=P("sta", win, None), check_vma=False
    )
```

```python
import math

import jax
import jax.numpy as jnp
from jax import lax
from jax.sharding import Mesh, PartitionSpec as P

LAGS = 1024
SMOOTH_HALF = 10


floor_level = 0.5


def shifted(value, axis, pairs):
    return lax.ppermute(value, axis, pairs)


def whiten(spectra, half_width):
    bin_count = spectra.shape[-1] // 2
    real_part = spectra[..., :bin_count].astype(jnp.float32)
    imag_part = spectra[..., bin_count:].astype(jnp.float32)
    amplitude = jnp.sqrt(real_part * real_part + imag_part * imag_part)
    padded = jnp.pad(amplitude, ((0, 0), (half_width, half_width)))
    taps = 2 * half_width + 1
    runs = {1: padded}
    width = 1
    while 2 * width <= taps:
        prior = runs[width]
        runs[2 * width] = prior[..., :-width] + prior[..., width:]
        width *= 2
    running = None
    start = 0
    for width in sorted(runs, reverse=True):
        if taps - start >= width:
            piece = runs[width][..., start : start + bin_count]
            running = piece if running is None else running + piece
            start += width
    smooth = running / (2 * half_width + 1)
    inverse = 1.0 / jnp.maximum(smooth, floor_level)
    return jnp.concatenate([real_part * inverse, imag_part * inverse], axis=-1).astype(jnp.bfloat16)


def owner_slots(owners, groups):
    flat_owner = owners.reshape(-1)
    count = flat_owner.shape[0]
    owner_hits = (flat_owner[:, None] == jnp.arange(groups, dtype=jnp.int32)[None, :]).astype(
        jnp.bfloat16
    )
    position = jnp.arange(count, dtype=jnp.int32)
    earlier = (position[None, :] < position[:, None]).astype(jnp.bfloat16)
    before = jnp.dot(earlier, owner_hits, preferred_element_type=jnp.float32)
    slot = jnp.sum(before * owner_hits.astype(jnp.float32), axis=1).astype(jnp.int32)
    return (flat_owner, slot)


def angle_tables(count, step, lag_count):
    period = 2 * 2048
    lag_value = jnp.arange(lag_count, dtype=jnp.int32) - lag_count // 2
    m = jnp.arange(count, dtype=jnp.int32)
    phase = jnp.mod((m * step)[:, None] * lag_value[None, :], period)
    angle = phase.astype(jnp.float32) * (2.0 * math.pi / period)
    return jnp.cos(angle), jnp.sin(angle)


def build_table(bin_count, lag_count, after):
    hi_step = 64
    hi_count = bin_count // hi_step
    cos_hi, sin_hi = angle_tables(hi_count, hi_step, lag_count)
    cos_lo, sin_lo = angle_tables(hi_step, 1, lag_count)
    cos_hi, sin_hi, cos_lo, sin_lo, _ = lax.optimization_barrier(
        (cos_hi, sin_hi, cos_lo, sin_lo, after)
    )
    frequency = jnp.arange(bin_count, dtype=jnp.int32).reshape(hi_count, hi_step, 1)
    weight = jnp.where(frequency == 0, 1.0, 2.0).astype(jnp.float32)
    cos_full = (cos_hi[:, None, :] * cos_lo[None, :, :] - sin_hi[:, None, :] * sin_lo[None, :, :]) * weight
    sin_full = (sin_hi[:, None, :] * cos_lo[None, :, :] + cos_hi[:, None, :] * sin_lo[None, :, :]) * weight
    cos_part = cos_full.astype(jnp.bfloat16).reshape(bin_count, lag_count)
    sin_part = (-sin_full).astype(jnp.bfloat16).reshape(bin_count, lag_count)
    return cos_part, sin_part


def select_rows(index, block):
    count = block.shape[0]
    chooser = (index[:, None] == jnp.arange(count, dtype=jnp.int32)[None, :]).astype(block.dtype)
    return jnp.dot(chooser, block, preferred_element_type=jnp.float32).astype(block.dtype)


def cross_rows(left_rows, right_rows):
    bin_count = left_rows.shape[-1] // 2
    left_real, left_imag = (left_rows[..., :bin_count], left_rows[..., bin_count:])
    right_real, right_imag = (right_rows[..., :bin_count], right_rows[..., bin_count:])
    real_cross = left_real * right_real + left_imag * right_imag
    imag_cross = left_imag * right_real - left_real * right_imag
    return real_cross.astype(jnp.bfloat16), imag_cross.astype(jnp.bfloat16)


def local(spectra, pair_first, pair_second, pair_owner):
    chips = lax.axis_size("wx")
    cores = lax.axis_size("wc")
    groups = chips * cores
    peers = lax.axis_size("sta")
    bin_count = spectra.shape[-1] // 2
    windows_all = spectra.shape[0] * groups
    factor = 1.0 / math.sqrt(2 * bin_count * windows_all)
    whitened = whiten(spectra[0], SMOOTH_HALF)
    first_rows = pair_first[0]
    second_rows = pair_second[0]
    offsets = first_rows.shape[0]

    z_pairs = [(i, (i - 2) % peers) for i in range(peers)]
    to_even = [(i, i - 1) for i in range(1, peers, 2)]
    to_odd = [(i, i + 1) for i in range(0, peers, 2)]
    rounds = offsets // 2
    chain = [whitened]
    for _ in range(rounds):
        chain.append(shifted(chain[-1], "sta", z_pairs))
    partner_rows = [None] * offsets
    for r in range(rounds + 1):
        partner_rows[2 * r] = select_rows(second_rows[2 * r], chain[r])
    table_after = None
    me = lax.axis_index("sta")
    is_odd = (me % 2) == 1
    last_odd = 2 * rounds - 1
    partner_index = shifted(
        jnp.stack([first_rows[last_odd], second_rows[last_odd]]), "sta", to_even
    )
    partner_first, partner_second = partner_index[0], partner_index[1]
    for m in range(rounds):
        from_odd = shifted(chain[m], "sta", to_even)
        if m == 0:
            partner_own = from_odd
        if m + 1 < rounds:
            from_even = shifted(chain[m + 1], "sta", to_odd)
            if m == 1:
                table_after = from_even
            partner_rows[2 * m + 1] = select_rows(second_rows[2 * m + 1], from_odd).astype(
                jnp.float32
            ) + select_rows(second_rows[2 * m + 1], from_even).astype(jnp.float32)
        else:
            partner_rows[2 * m + 1] = select_rows(second_rows[2 * m + 1], from_odd)

    cos_table, sin_table = build_table(bin_count, LAGS, table_after)
    pair_count = first_rows.shape[1]
    own_all = select_rows(first_rows.reshape(-1), whitened)
    pieces = []
    for offset_step in range(offsets):
        own_rows = own_all[offset_step * pair_count : (offset_step + 1) * pair_count]
        pieces.append(
            cross_rows(own_rows.astype(jnp.float32), partner_rows[offset_step].astype(jnp.float32))
        )
    real_value = jnp.concatenate([piece[0] for piece in pieces], axis=0)
    imag_value = jnp.concatenate([piece[1] for piece in pieces], axis=0)
    transformed = (
        (
            jnp.dot(real_value, cos_table, preferred_element_type=jnp.float32)
            + jnp.dot(imag_value, sin_table, preferred_element_type=jnp.float32)
        )
        * factor
    ).astype(jnp.bfloat16)
    transformed = lax.optimization_barrier(transformed)
    help_real, help_imag = cross_rows(
        select_rows(partner_first, partner_own).astype(jnp.float32),
        select_rows(partner_second, chain[rounds]).astype(jnp.float32),
    )
    helped = (
        (
            jnp.dot(help_real, cos_table, preferred_element_type=jnp.float32)
            + jnp.dot(help_imag, sin_table, preferred_element_type=jnp.float32)
        )
        * factor
    ).astype(jnp.bfloat16)
    helped = shifted(helped, "sta", to_odd)
    late_rows = slice(last_odd * pair_count, (last_odd + 1) * pair_count)
    transformed = transformed.at[late_rows].set(
        jnp.where(is_odd, helped, transformed[late_rows])
    )
    pair_rows = real_value.shape[0]
    capacity = 2 * pair_rows // groups
    padded_capacity = -(-capacity // 8) * 8
    owner_row, _ = lax.optimization_barrier((pair_owner[0], chain[2]))
    owners, slot_of = owner_slots(owner_row, groups)
    my_core = lax.axis_index("wc")
    local_row = (owners // cores) * padded_capacity + slot_of
    slot_index = jnp.arange(chips * padded_capacity, dtype=jnp.int32)[:, None]
    own_target = jnp.where(owners % cores == my_core, local_row, -1)
    other_target = jnp.where(owners % cores == my_core, -1, local_row)

    def placed(row_target):
        chooser = (row_target[None, :] == slot_index).astype(jnp.bfloat16)
        return jnp.dot(chooser, transformed, preferred_element_type=jnp.float32).astype(
            jnp.bfloat16
        )

    from_other_core = lax.ppermute(placed(other_target), "wc", [(0, 1), (1, 0)])
    chip_sum = (placed(own_target).astype(jnp.float32) + from_other_core.astype(jnp.float32))
    chip_sum = chip_sum.astype(jnp.bfloat16).reshape(chips, padded_capacity, LAGS)
    received = lax.all_to_all(chip_sum, "wx", split_axis=0, concat_axis=0, tiled=True)
    result = jnp.sum(received[:, :capacity].astype(jnp.float32), axis=0).astype(jnp.bfloat16)
    return result[None]


def solution(mesh):
    sta_count, win_count = mesh.devices.shape
    split_mesh = Mesh(mesh.devices.reshape(sta_count, win_count // 2, 2), ("sta", "wx", "wc"))
    win = ("wx", "wc")
    placed = (
        P(win, "sta", None),
        P("sta", None, None),
        P("sta", None, None),
        P("sta", None, None),
    )
    return jax.shard_map(
        local, mesh=split_mesh, in_specs=placed, out_specs=P("sta", win, None), check_vma=False
    )
```
